768 devices in a mesh: gx: 24 (over x, z_hi, core), gy: 32 (over z_lo, y).
Axes of the slice: x: 4, y: 8, z: 12 (z_hi: 3, z_lo: 4; z = z_hi * 4 + z_lo), core: 2. Of those that a mesh axis runs over, the one named last changes fastest.
Arguments:
- state: float32 [10, 192, 256, 128], P(None, 'gx', 'gy'), may hold values from 0.01 to 3, as said below
- source_in: float32 [10, 192, 256, 128], P(None, 'gx', 'gy'), may hold values from -3 to 3
- counts: int32 [192, 256], P('gx', 'gy'), may hold values from 1 to 8, as said below
- diffusivity: float32 [10], replicated, may hold values from 0.3 to 1
- log_rate: float32 [21], replicated, may hold values from 0.3 to 1
- activation: float32 [21], replicated, may hold values from 0.4 to 0.8
- heat_release: float32 [21], replicated, may hold values from -1 to 2
Outputs:
- next_state: float32 [10, 192, 256, 128], P(None, 'gx', 'gy')
- late_source: float32 [10, 192, 256, 128], P(None, 'gx', 'gy')
The draws below stay inside these ranges and needn't reach their ends.
Inputs may be any that keep to these rules, and one draw needn't show every extreme that they name: Boxes of 8 x 8 blocks are either flame boxes, about an eighth of them, where every count is 5 or more and one is 8, or others, where counts are 1 or 2. `state`: rows 0 to 8 lie in [0.01, 1]; the last row lies in [1, 3].
All inputs are finite; a program needn't handle non-finite values.
Results may differ from the reference program's by a relative error of at most 0.0003.
Values sent between devices are 32-bit elements; how exact they have to be, the bound alone decides.
No kernel may reach another device: no remote copies, remote signals or barrier semaphores. Data moves between devices by JAX's collectives and lax.ppermute only.
A program may use at most 32 MiB of HBM per device.

```python
import math
import jax
import jax.numpy as jnp
import numpy as np
from jax import lax

SPECIES = 9
REACTIONS = 21
CMAX = 8
CX = 8
CY = 8
CZ = 128
NX = 192
NY = 256


def draw_state(key, part):
    first_key, second_key = jax.random.split(key)
    species = jax.random.uniform(first_key, (SPECIES, NX, NY, CZ), jnp.float32, 0.05, 1.0)
    temper = jax.random.uniform(second_key, (1, NX, NY, CZ), jnp.float32, 1.0, 3.0)
    return jnp.concatenate([species, temper], 0).astype(jnp.float32)


def draw_counts(key, part):
    boxes_x = NX // CX
    boxes_y = NY // CY
    perm_key, base_key, flame_key = jax.random.split(key, 3)
    ranking = jax.random.permutation(perm_key, boxes_x * boxes_y).reshape(boxes_x, boxes_y)
    flame_box = ranking < max(1, boxes_x * boxes_y // 8)
    flame = jnp.repeat(jnp.repeat(flame_box, CX, 0), CY, 1)
    base = jax.random.randint(base_key, (NX, NY), 1, 3)
    heated = jax.random.randint(flame_key, (NX, NY), 5, CMAX + 1)
    row_index = jnp.arange(NX)[:, None] % CX
    col_index = jnp.arange(NY)[None, :] % CY
    corner = (row_index == 0) & (col_index == 0)
    heated = jnp.where(corner, CMAX, heated)
    return jnp.where(flame, heated, base).astype(jnp.int32)


def shard_levels(own_key, shape, shards, smallest, high):
    loudness = 1.0
    for position, parts in shards:
        steps = jax.random.uniform(jax.random.fold_in(jax.random.fold_in(own_key, 6), position), (parts,), jnp.float32, smallest / len(shards), high / len(shards))
        loudness = loudness * jnp.repeat(jnp.exp(steps), shape[position] // parts).reshape((-1,) + (1,) * (len(shape) - 1 - position))
    return loudness


def centred(rng, dims, scale, limit, cuts=(), kind=jnp.bfloat16):
    level = shard_levels(rng, dims, cuts, -0.22, 0.18) if cuts else 1.0
    result = jax.random.normal(rng, dims, jnp.float32) * scale * level
    return jnp.minimum(jnp.maximum(result, -limit), limit).astype(kind)


def setup_inputs(seed: int = 0) -> dict:
    splits = jax.random.split(jax.random.key(seed), 8)
    state = draw_state(jax.random.fold_in(splits[7], 71), 0)
    source_in = centred(splits[1], (SPECIES + 1, NX, NY, CZ), 1.0, 3.0, ((1, 24), (2, 32)), jnp.float32)
    counts = draw_counts(jax.random.fold_in(splits[7], 71), 0)
    diffusivity = jnp.clip(jnp.exp(jax.random.uniform(splits[3], (SPECIES + 1,), jnp.float32, math.log(0.3), math.log(1.0))), 0.3, 1.0)
    log_rate = jnp.clip(jax.random.uniform(splits[4], (REACTIONS,), jnp.float32, 0.3, 1.0), 0.3, 1.0)
    activation = jnp.clip(jax.random.uniform(splits[5], (REACTIONS,), jnp.float32, 0.4, 0.8), 0.4, 0.8)
    heat_release = jnp.clip(jax.random.uniform(splits[6], (REACTIONS,), jnp.float32, -1.0, 2.0), -1.0, 2.0)
    return {"state": state, "source_in": source_in, "counts": counts, "diffusivity": diffusivity, "log_rate": log_rate, "activation": activation, "heat_release": heat_release}


time_step = 0.15

reaction_table = (
    (3, 1, (4, 5)), (4, 0, (3, 5)), (5, 0, (3, 2)), (5, 5, (4, 2)),
    (3, 3, (0,)), (3, 5, (2,)), (4, 4, (1,)), (3, 4, (5,)), (3, 1, (6,)),
    (6, 3, (0, 1)), (6, 3, (5, 5)), (6, 4, (1, 5)), (6, 5, (2, 1)),
    (6, 6, (7, 1)), (7, 9, (5, 5)), (7, 3, (2, 5)), (7, 3, (6, 0)),
    (7, 4, (5, 6)), (7, 5, (6, 2)), (0, 9, (3, 3)), (2, 9, (3, 5)),
)


def tables(heat_release):
    leading = np.zeros((21, 10), np.float32)
    trailing = np.zeros((21, 10), np.float32)
    change = np.zeros((9, 21), np.float32)
    for reaction, entry in enumerate(reaction_table):
        leading[reaction, entry[0]] = 1.0
        trailing[reaction, entry[1]] = 1.0
        change[entry[0], reaction] -= 1.0
        if entry[1] < 9:
            change[entry[1], reaction] -= 1.0
        for product in entry[2]:
            change[product, reaction] += 1.0
    matrix = jnp.concatenate([jnp.asarray(change).astype(jnp.float32), heat_release[None, :]], 0)
    return jnp.asarray(leading).astype(jnp.float32), jnp.asarray(trailing).astype(jnp.float32), matrix


def advance(current, coeffs, stride, active, leading, trailing, matrix):
    augmented = jnp.concatenate([current[:9], jnp.ones_like(current[:1])], 0)
    reactant_one = jnp.dot(leading, augmented, precision=lax.Precision.HIGHEST)
    reactant_two = jnp.dot(trailing, augmented, precision=lax.Precision.HIGHEST)
    rate_terms = coeffs * reactant_one * reactant_two
    change_now = jnp.dot(matrix, rate_terms, precision=lax.Precision.HIGHEST)
    return jnp.where(active[None, :], current + stride[None, :] * change_now, current)


def chemistry(fields_in, counts, log_rate, activation, heat_release):
    leading, trailing, matrix = tables(heat_release)

    def one_slice(pieces):
        slab, slab_counts = pieces
        cell_rows = slab.reshape(slab.shape[0], slab.shape[1] * slab.shape[2])
        counts_cells = jnp.repeat(slab_counts, slab.shape[2])
        coeffs = jnp.exp(log_rate[:, None] - activation[:, None] / cell_rows[9][None, :])
        stride = time_step / counts_cells.astype(jnp.float32)
        current = cell_rows
        for turn_index in range(CMAX):
            current = advance(current, coeffs, stride, turn_index < counts_cells, leading, trailing, matrix)
        return ((current - cell_rows) / time_step).reshape(slab.shape)

    slabs = lax.map(one_slice, (jnp.moveaxis(fields_in, 1, 0), counts))
    return jnp.moveaxis(slabs, 0, 1)


def laplace(field):
    beside = jnp.roll(field, 1, 1) + jnp.roll(field, -1, 1)
    beside = beside + jnp.roll(field, 1, 2) + jnp.roll(field, -1, 2)
    beside = beside + jnp.roll(field, 1, 3) + jnp.roll(field, -1, 3)
    return beside - 6.0 * field


def reference(state, source_in, counts, diffusivity, log_rate, activation, heat_release):
    spread = diffusivity[:, None, None, None]
    first_section = state + time_step * (spread * laplace(state) + source_in)
    early = chemistry(state, counts, log_rate, activation, heat_release)
    next_state = 0.5 * state + 0.5 * (first_section + time_step * (spread * laplace(first_section) + early))
    late_source = chemistry(first_section, counts, log_rate, activation, heat_release)
    return next_state, late_source
```

```python
import jax
import jax.numpy as jnp
import numpy as np
from jax import lax
from jax.experimental import pallas as pl
from jax.experimental.pallas import tpu as pltpu
from jax.sharding import PartitionSpec as P

time_step = 0.15
reaction_table = (
    (3, 1, (4, 5)),
    (4, 0, (3, 5)),
    (5, 0, (3, 2)),
    (5, 5, (4, 2)),
    (3, 3, (0,)),
    (3, 5, (2,)),
    (4, 4, (1,)),
    (3, 4, (5,)),
    (3, 1, (6,)),
    (6, 3, (0, 1)),
    (6, 3, (5, 5)),
    (6, 4, (1, 5)),
    (6, 5, (2, 1)),
    (6, 6, (7, 1)),
    (7, 9, (5, 5)),
    (7, 3, (2, 5)),
    (7, 3, (6, 0)),
    (7, 4, (5, 6)),
    (7, 5, (6, 2)),
    (0, 9, (3, 3)),
    (2, 9, (3, 5)),
)
SPECIES = 9
CMAX = 8


def stoichiometry():
    change = np.zeros((SPECIES, len(reaction_table)), np.int64)
    for reaction, entry in enumerate(reaction_table):
        change[entry[0], reaction] -= 1
        if entry[1] < SPECIES:
            change[entry[1], reaction] -= 1
        for product in entry[2]:
            change[product, reaction] += 1
    return change


def chem_kernel(rate_ref, act_ref, heat_ref, u_ref, cnt_ref, o_ref):
    change = stoichiometry()
    reactions = len(reaction_table)
    rows = u_ref.shape[0]

    def per_x(x, carry):
        start = [u_ref[s, x] for s in range(rows)]
        temper = start[rows - 1]
        coeffs = [jnp.exp(rate_ref[r] - act_ref[r] / temper) for r in range(reactions)]
        heat = [heat_ref[r] for r in range(reactions)]
        cnt = cnt_ref[x]
        stride = time_step / cnt.astype(jnp.float32)
        cur = list(start)
        for turn in range(CMAX):
            active = turn < cnt
            rates = []
            for r, entry in enumerate(reaction_table):
                term = coeffs[r] * cur[entry[0]]
                if entry[1] < SPECIES:
                    term = term * cur[entry[1]]
                rates.append(term)
            new = []
            for s in range(SPECIES):
                total = None
                for r in range(reactions):
                    c = int(change[s, r])
                    if c == 0:
                        continue
                    piece = rates[r] if abs(c) == 1 else rates[r] * float(abs(c))
                    if total is None:
                        total = piece if c > 0 else -piece
                    elif c > 0:
                        total = total + piece
                    else:
                        total = total - piece
                if total is None:
                    new.append(cur[s])
                else:
                    new.append(jnp.where(active, cur[s] + stride * total, cur[s]))
            heat_total = heat[0] * rates[0]
            for r in range(1, reactions):
                heat_total = heat_total + heat[r] * rates[r]
            new.append(jnp.where(active, cur[SPECIES] + stride * heat_total, cur[SPECIES]))
            cur = new
        for s in range(rows):
            o_ref[s, x] = (cur[s] - start[s]) / time_step
        return carry

    lax.fori_loop(0, u_ref.shape[1], per_x, 0)


def chemistry(fields, cell_counts, log_rate, activation, heat_release):
    smem = pl.BlockSpec(memory_space=pltpu.SMEM)
    vmem = pl.BlockSpec(memory_space=pltpu.VMEM)
    return pl.pallas_call(
        chem_kernel,
        out_shape=jax.ShapeDtypeStruct(fields.shape, jnp.float32),
        in_specs=[smem, smem, smem, vmem, vmem],
        out_specs=vmem,
    )(log_rate, activation, heat_release, fields, cell_counts)


def shift_pairs(size, step):
    return [(i, (i + step) % size) for i in range(size)]


def diag_pairs(nx, ny, sx, sy):
    return [
        (i * ny + j, ((i + sx) % nx) * ny + (j + sy) % ny)
        for i in range(nx)
        for j in range(ny)
    ]


def laplace_parts(s, lo, hi):
    c = s[:, lo:hi, lo:hi]
    beside = s[:, lo - 1:hi - 1, lo:hi] + s[:, lo + 1:hi + 1, lo:hi]
    beside = beside + s[:, lo:hi, lo - 1:hi - 1] + s[:, lo:hi, lo + 1:hi + 1]
    beside = beside + jnp.roll(c, 1, 3) + jnp.roll(c, -1, 3)
    return beside - 6.0 * c


def local(state, source_in, counts, diffusivity, log_rate, activation, heat_release):
    nx = lax.axis_size("gx")
    ny = lax.axis_size("gy")
    rows, cx, cy, cz = state.shape
    spread = diffusivity[:, None, None, None]
    cell_counts = jnp.broadcast_to(counts[:, :, None], (cx, cy, cz))

    to_xp = jnp.concatenate([state[:, cx - 2:], source_in[:, cx - 1:]], 1)
    to_xm = jnp.concatenate([state[:, :2], source_in[:, :1]], 1)
    to_yp = jnp.concatenate([state[:, :, cy - 2:], source_in[:, :, cy - 1:]], 2)
    to_ym = jnp.concatenate([state[:, :, :2], source_in[:, :, :1]], 2)
    from_xm = lax.ppermute(to_xp, "gx", shift_pairs(nx, 1))
    from_xp = lax.ppermute(to_xm, "gx", shift_pairs(nx, -1))
    from_ym = lax.ppermute(to_yp, "gy", shift_pairs(ny, 1))
    from_yp = lax.ppermute(to_ym, "gy", shift_pairs(ny, -1))
    both = ("gx", "gy")
    c_mm = lax.ppermute(state[:, cx - 1:, cy - 1:], both, diag_pairs(nx, ny, 1, 1))
    c_mp = lax.ppermute(state[:, cx - 1:, :1], both, diag_pairs(nx, ny, 1, -1))
    c_pm = lax.ppermute(state[:, :1, cy - 1:], both, diag_pairs(nx, ny, -1, 1))
    c_pp = lax.ppermute(state[:, :1, :1], both, diag_pairs(nx, ny, -1, -1))

    early = chemistry(state, cell_counts, log_rate, activation, heat_release)

    def zeros(a, b):
        return jnp.zeros((rows, a, b, cz), jnp.float32)

    s_xm, q_xm = from_xm[:, :2], from_xm[:, 2:]
    s_xp, q_xp = from_xp[:, :2], from_xp[:, 2:]
    s_ym, q_ym = from_ym[:, :, :2], from_ym[:, :, 2:]
    s_yp, q_yp = from_yp[:, :, :2], from_yp[:, :, 2:]
    ext = jnp.concatenate(
        [
            jnp.concatenate([zeros(1, 2), s_xm[:, :1], zeros(1, 2)], 2),
            jnp.concatenate([zeros(1, 1), c_mm, s_xm[:, 1:], c_mp, zeros(1, 1)], 2),
            jnp.concatenate([s_ym, state, s_yp], 2),
            jnp.concatenate([zeros(1, 1), c_pm, s_xp[:, :1], c_pp, zeros(1, 1)], 2),
            jnp.concatenate([zeros(1, 2), s_xp[:, 1:], zeros(1, 2)], 2),
        ],
        1,
    )
    src = jnp.concatenate(
        [
            jnp.concatenate([zeros(1, 1), q_xm, zeros(1, 1)], 2),
            jnp.concatenate([q_ym, source_in, q_yp], 2),
            jnp.concatenate([zeros(1, 1), q_xp, zeros(1, 1)], 2),
        ],
        1,
    )
    first_ext = ext[:, 1:-1, 1:-1] + time_step * (
        spread * laplace_parts(ext, 1, cx + 3) + src
    )
    first_section = first_ext[:, 1:-1, 1:-1]
    next_state = 0.5 * state + 0.5 * (
        first_section + time_step * (spread * laplace_parts(first_ext, 1, cx + 1) + early)
    )
    late_source = chemistry(first_section, cell_counts, log_rate, activation, heat_release)
    return (next_state, late_source)


def solution(mesh):
    in_specs = (
        P(None, "gx", "gy", None),
        P(None, "gx", "gy", None),
        P("gx", "gy"),
        P(),
        P(),
        P(),
        P(),
    )
    out_specs = (P(None, "gx", "gy", None), P(None, "gx", "gy", None))
    return jax.shard_map(local, mesh=mesh, in_specs=in_specs, out_specs=out_specs, check_vma=False)
```

```python
import jax
import jax.numpy as jnp
import numpy as np
from jax import lax
from jax.experimental import pallas as pl
from jax.experimental.pallas import tpu as pltpu
from jax.sharding import PartitionSpec as P

time_step = 0.15
reaction_table = (
    (3, 1, (4, 5)),
    (4, 0, (3, 5)),
    (5, 0, (3, 2)),
    (5, 5, (4, 2)),
    (3, 3, (0,)),
    (3, 5, (2,)),
    (4, 4, (1,)),
    (3, 4, (5,)),
    (3, 1, (6,)),
    (6, 3, (0, 1)),
    (6, 3, (5, 5)),
    (6, 4, (1, 5)),
    (6, 5, (2, 1)),
    (6, 6, (7, 1)),
    (7, 9, (5, 5)),
    (7, 3, (2, 5)),
    (7, 3, (6, 0)),
    (7, 4, (5, 6)),
    (7, 5, (6, 2)),
    (0, 9, (3, 3)),
    (2, 9, (3, 5)),
)
SPECIES = 9
CMAX = 8


def stoichiometry():
    change = np.zeros((SPECIES, len(reaction_table)), np.int64)
    for reaction, entry in enumerate(reaction_table):
        change[entry[0], reaction] -= 1
        if entry[1] < SPECIES:
            change[entry[1], reaction] -= 1
        for product in entry[2]:
            change[product, reaction] += 1
    return change


def chem_kernel(rate_ref, act_ref, heat_ref, u_ref, cnt_ref, o_ref):
    change = stoichiometry()
    reactions = len(reaction_table)
    rows = u_ref.shape[0]

    def per_x(x, carry):
        start = [u_ref[s, x] for s in range(rows)]
        temper = start[rows - 1]
        coeffs = [jnp.exp(rate_ref[r] - act_ref[r] / temper) for r in range(reactions)]
        heat = [heat_ref[r] for r in range(reactions)]
        cnt = cnt_ref[x]
        stride = time_step / cnt.astype(jnp.float32)
        cur = list(start)
        for turn in range(CMAX):
            active = turn < cnt
            rates = []
            for r, entry in enumerate(reaction_table):
                term = coeffs[r] * cur[entry[0]]
                if entry[1] < SPECIES:
                    term = term * cur[entry[1]]
                rates.append(term)
            new = []
            for s in range(SPECIES):
                total = None
                for r in range(reactions):
                    c = int(change[s, r])
                    if c == 0:
                        continue
                    piece = rates[r] if abs(c) == 1 else rates[r] * float(abs(c))
                    if total is None:
                        total = piece if c > 0 else -piece
                    elif c > 0:
                        total = total + piece
                    else:
                        total = total - piece
                if total is None:
                    new.append(cur[s])
                else:
                    new.append(jnp.where(active, cur[s] + stride * total, cur[s]))
            heat_total = heat[0] * rates[0]
            for r in range(1, reactions):
                heat_total = heat_total + heat[r] * rates[r]
            new.append(jnp.where(active, cur[SPECIES] + stride * heat_total, cur[SPECIES]))
            cur = new
        for s in range(rows):
            o_ref[s, x] = (cur[s] - start[s]) / time_step
        return carry

    lax.fori_loop(0, u_ref.shape[1], per_x, 0)


def chemistry(fields, cell_counts, log_rate, activation, heat_release):
    smem = pl.BlockSpec(memory_space=pltpu.SMEM)
    vmem = pl.BlockSpec(memory_space=pltpu.VMEM)
    return pl.pallas_call(
        chem_kernel,
        out_shape=jax.ShapeDtypeStruct(fields.shape, jnp.float32),
        in_specs=[smem, smem, smem, vmem, vmem],
        out_specs=vmem,
    )(log_rate, activation, heat_release, fields, cell_counts)


def shift_pairs(size, step):
    return [(i, (i + step) % size) for i in range(size)]


def laplace_parts(s, lo, hi):
    c = s[:, lo:hi, lo:hi]
    beside = s[:, lo - 1:hi - 1, lo:hi] + s[:, lo + 1:hi + 1, lo:hi]
    beside = beside + s[:, lo:hi, lo - 1:hi - 1] + s[:, lo:hi, lo + 1:hi + 1]
    beside = beside + jnp.roll(c, 1, 3) + jnp.roll(c, -1, 3)
    return beside - 6.0 * c


def local(state, source_in, counts, diffusivity, log_rate, activation, heat_release):
    nx = lax.axis_size("gx")
    ny = lax.axis_size("gy")
    rows, cx, cy, cz = state.shape
    spread = diffusivity[:, None, None, None]
    cell_counts = jnp.broadcast_to(counts[:, :, None], (cx, cy, cz))

    to_yp = jnp.concatenate([state[:, :, cy - 2:], source_in[:, :, cy - 1:]], 2)
    to_ym = jnp.concatenate([state[:, :, :2], source_in[:, :, :1]], 2)
    from_ym = lax.ppermute(to_yp, "gy", shift_pairs(ny, 1))
    from_yp = lax.ppermute(to_ym, "gy", shift_pairs(ny, -1))

    early = chemistry(state, cell_counts, log_rate, activation, heat_release)

    def zeros(a, b):
        return jnp.zeros((rows, a, b, cz), jnp.float32)

    wide = jnp.concatenate([from_ym[:, :, :2], state, from_yp[:, :, :2]], 2)
    wide_src = jnp.concatenate(
        [zeros(cx, 1), from_ym[:, :, 2:], source_in, from_yp[:, :, 2:], zeros(cx, 1)], 2
    )
    to_xp = jnp.concatenate([wide[:, cx - 2:], wide_src[:, cx - 1:]], 1)
    to_xm = jnp.concatenate([wide[:, :2], wide_src[:, :1]], 1)
    from_xm = lax.ppermute(to_xp, "gx", shift_pairs(nx, 1))
    from_xp = lax.ppermute(to_xm, "gx", shift_pairs(nx, -1))
    ext = jnp.concatenate([from_xm[:, :2], wide, from_xp[:, :2]], 1)
    src = jnp.concatenate([from_xm[:, 2:], wide_src, from_xp[:, 2:]], 1)[:, :, 1:-1]
    first_ext = ext[:, 1:-1, 1:-1] + time_step * (
        spread * laplace_parts(ext, 1, cx + 3) + src
    )
    first_section = first_ext[:, 1:-1, 1:-1]
    next_state = 0.5 * state + 0.5 * (
        first_section + time_step * (spread * laplace_parts(first_ext, 1, cx + 1) + early)
    )
    late_source = chemistry(first_section, cell_counts, log_rate, activation, heat_release)
    return (next_state, late_source)


def solution(mesh):
    in_specs = (
        P(None, "gx", "gy", None),
        P(None, "gx", "gy", None),
        P("gx", "gy"),
        P(),
        P(),
        P(),
        P(),
    )
    out_specs = (P(None, "gx", "gy", None), P(None, "gx", "gy", None))
    return jax.shard_map(local, mesh=mesh, in_specs=in_specs, out_specs=out_specs, check_vma=False)
```

```python
import jax
import jax.numpy as jnp
import numpy as np
from jax import lax
from jax.experimental import pallas as pl
from jax.experimental.pallas import tpu as pltpu
from jax.sharding import PartitionSpec as P

time_step = 0.15
reaction_table = (
    (3, 1, (4, 5)),
    (4, 0, (3, 5)),
    (5, 0, (3, 2)),
    (5, 5, (4, 2)),
    (3, 3, (0,)),
    (3, 5, (2,)),
    (4, 4, (1,)),
    (3, 4, (5,)),
    (3, 1, (6,)),
    (6, 3, (0, 1)),
    (6, 3, (5, 5)),
    (6, 4, (1, 5)),
    (6, 5, (2, 1)),
    (6, 6, (7, 1)),
    (7, 9, (5, 5)),
    (7, 3, (2, 5)),
    (7, 3, (6, 0)),
    (7, 4, (5, 6)),
    (7, 5, (6, 2)),
    (0, 9, (3, 3)),
    (2, 9, (3, 5)),
)
SPECIES = 9
CMAX = 8


def stoichiometry():
    change = np.zeros((SPECIES, len(reaction_table)), np.int64)
    for reaction, entry in enumerate(reaction_table):
        change[entry[0], reaction] -= 1
        if entry[1] < SPECIES:
            change[entry[1], reaction] -= 1
        for product in entry[2]:
            change[product, reaction] += 1
    return change


def chem_kernel(rate_ref, act_ref, heat_ref, u_ref, cnt_ref, o_ref):
    change = stoichiometry()
    reactions = len(reaction_table)
    rows = u_ref.shape[0]

    def per_x(x, carry):
        start = [u_ref[s, x] for s in range(rows)]
        temper = start[rows - 1]
        coeffs = [jnp.exp(rate_ref[r] - act_ref[r] / temper) for r in range(reactions)]
        heat = [heat_ref[r] for r in range(reactions)]
        cnt = cnt_ref[x]
        stride = time_step / cnt.astype(jnp.float32)
        cur = list(start)
        for turn in range(CMAX):
            active = turn < cnt
            rates = []
            for r, entry in enumerate(reaction_table):
                term = coeffs[r] * cur[entry[0]]
                if entry[1] < SPECIES:
                    term = term * cur[entry[1]]
                rates.append(term)
            new = []
            for s in range(SPECIES):
                total = None
                for r in range(reactions):
                    c = int(change[s, r])
                    if c == 0:
                        continue
                    piece = rates[r] if abs(c) == 1 else rates[r] * float(abs(c))
                    if total is None:
                        total = piece if c > 0 else -piece
                    elif c > 0:
                        total = total + piece
                    else:
                        total = total - piece
                if total is None:
                    new.append(cur[s])
                else:
                    new.append(jnp.where(active, cur[s] + stride * total, cur[s]))
            heat_total = heat[0] * rates[0]
            for r in range(1, reactions):
                heat_total = heat_total + heat[r] * rates[r]
            new.append(jnp.where(active, cur[SPECIES] + stride * heat_total, cur[SPECIES]))
            cur = new
        for s in range(rows):
            o_ref[s, x] = (cur[s] - start[s]) / time_step
        return carry

    lax.fori_loop(0, u_ref.shape[1], per_x, 0)


def chemistry(fields, cell_counts, log_rate, activation, heat_release):
    smem = pl.BlockSpec(memory_space=pltpu.SMEM)
    vmem = pl.BlockSpec(memory_space=pltpu.VMEM)
    return pl.pallas_call(
        chem_kernel,
        out_shape=jax.ShapeDtypeStruct(fields.shape, jnp.float32),
        in_specs=[smem, smem, smem, vmem, vmem],
        out_specs=vmem,
    )(log_rate, activation, heat_release, fields, cell_counts)


def shift_pairs(size, step):
    return [(i, (i + step) % size) for i in range(size)]


def exchange(to_lo, to_hi, axis, size):
    if size % 2:
        from_lo = lax.ppermute(to_hi, axis, shift_pairs(size, 1))
        from_hi = lax.ppermute(to_lo, axis, shift_pairs(size, -1))
        return from_lo, from_hi
    even = lax.axis_index(axis) % 2 == 0
    inner = [(i, i + 1 if i % 2 == 0 else i - 1) for i in range(size)]
    outer = [(i, (i - 1) % size if i % 2 == 0 else (i + 1) % size) for i in range(size)]
    first = lax.ppermute(jnp.where(even, to_hi, to_lo), axis, inner)
    second = lax.ppermute(jnp.where(even, to_lo, to_hi), axis, outer)
    return jnp.where(even, second, first), jnp.where(even, first, second)


def laplace_parts(s, lo, hi):
    c = s[:, lo:hi, lo:hi]
    beside = s[:, lo - 1:hi - 1, lo:hi] + s[:, lo + 1:hi + 1, lo:hi]
    beside = beside + s[:, lo:hi, lo - 1:hi - 1] + s[:, lo:hi, lo + 1:hi + 1]
    beside = beside + jnp.roll(c, 1, 3) + jnp.roll(c, -1, 3)
    return beside - 6.0 * c


def local(state, source_in, counts, diffusivity, log_rate, activation, heat_release):
    nx = lax.axis_size("gx")
    ny = lax.axis_size("gy")
    rows, cx, cy, cz = state.shape
    spread = diffusivity[:, None, None, None]
    cell_counts = jnp.broadcast_to(counts[:, :, None], (cx, cy, cz))

    to_yp = jnp.concatenate([state[:, :, cy - 2:], source_in[:, :, cy - 1:]], 2)
    to_ym = jnp.concatenate([state[:, :, :2], source_in[:, :, :1]], 2)
    from_ym, from_yp = exchange(to_ym, to_yp, "gy", ny)

    early = chemistry(state, cell_counts, log_rate, activation, heat_release)

    def zeros(a, b):
        return jnp.zeros((rows, a, b, cz), jnp.float32)

    wide = jnp.concatenate([from_ym[:, :, :2], state, from_yp[:, :, :2]], 2)
    wide_src = jnp.concatenate(
        [zeros(cx, 1), from_ym[:, :, 2:], source_in, from_yp[:, :, 2:], zeros(cx, 1)], 2
    )
    to_xp = jnp.concatenate([wide[:, cx - 2:], wide_src[:, cx - 1:]], 1)
    to_xm = jnp.concatenate([wide[:, :2], wide_src[:, :1]], 1)
    from_xm, from_xp = exchange(to_xm, to_xp, "gx", nx)
    ext = jnp.concatenate([from_xm[:, :2], wide, from_xp[:, :2]], 1)
    src = jnp.concatenate([from_xm[:, 2:], wide_src, from_xp[:, 2:]], 1)[:, :, 1:-1]
    first_ext = ext[:, 1:-1, 1:-1] + time_step * (
        spread * laplace_parts(ext, 1, cx + 3) + src
    )
    first_section = first_ext[:, 1:-1, 1:-1]
    next_state = 0.5 * state + 0.5 * (
        first_section + time_step * (spread * laplace_parts(first_ext, 1, cx + 1) + early)
    )
    late_source = chemistry(first_section, cell_counts, log_rate, activation, heat_release)
    return (next_state, late_source)


def solution(mesh):
    in_specs = (
        P(None, "gx", "gy", None),
        P(None, "gx", "gy", None),
        P("gx", "gy"),
        P(),
        P(),
        P(),
        P(),
    )
    out_specs = (P(None, "gx", "gy", None), P(None, "gx", "gy", None))
    return jax.shard_map(local, mesh=mesh, in_specs=in_specs, out_specs=out_specs, check_vma=False)
```

```python
import jax
import jax.numpy as jnp
import numpy as np
from jax import lax
from jax.experimental import pallas as pl
from jax.experimental.pallas import tpu as pltpu
from jax.sharding import PartitionSpec as P

time_step = 0.15
reaction_table = (
    (3, 1, (4, 5)),
    (4, 0, (3, 5)),
    (5, 0, (3, 2)),
    (5, 5, (4, 2)),
    (3, 3, (0,)),
    (3, 5, (2,)),
    (4, 4, (1,)),
    (3, 4, (5,)),
    (3, 1, (6,)),
    (6, 3, (0, 1)),
    (6, 3, (5, 5)),
    (6, 4, (1, 5)),
    (6, 5, (2, 1)),
    (6, 6, (7, 1)),
    (7, 9, (5, 5)),
    (7, 3, (2, 5)),
    (7, 3, (6, 0)),
    (7, 4, (5, 6)),
    (7, 5, (6, 2)),
    (0, 9, (3, 3)),
    (2, 9, (3, 5)),
)
SPECIES = 9
CMAX = 8


def stoichiometry():
    change = np.zeros((SPECIES, len(reaction_table)), np.int64)
    for reaction, entry in enumerate(reaction_table):
        change[entry[0], reaction] -= 1
        if entry[1] < SPECIES:
            change[entry[1], reaction] -= 1
        for product in entry[2]:
            change[product, reaction] += 1
    return change


def chem_kernel(rate_ref, act_ref, heat_ref, u_ref, cnt_ref, o_ref):
    change = stoichiometry()
    reactions = len(reaction_table)
    rows = u_ref.shape[0]

    def per_x(x, carry):
        start = [u_ref[s, x] for s in range(rows)]
        temper = start[rows - 1]
        coeffs = [jnp.exp(rate_ref[r] - act_ref[r] / temper) for r in range(reactions)]
        heat = [heat_ref[r] for r in range(reactions)]
        cnt = cnt_ref[x]
        stride = time_step / cnt.astype(jnp.float32)
        cur = list(start)
        for turn in range(CMAX):
            active = turn < cnt
            rates = []
            for r, entry in enumerate(reaction_table):
                term = coeffs[r] * cur[entry[0]]
                if entry[1] < SPECIES:
                    term = term * cur[entry[1]]
                rates.append(term)
            new = []
            for s in range(SPECIES):
                total = None
                for r in range(reactions):
                    c = int(change[s, r])
                    if c == 0:
                        continue
                    piece = rates[r] if abs(c) == 1 else rates[r] * float(abs(c))
                    if total is None:
                        total = piece if c > 0 else -piece
                    elif c > 0:
                        total = total + piece
                    else:
                        total = total - piece
                if total is None:
                    new.append(cur[s])
                else:
                    new.append(jnp.where(active, cur[s] + stride * total, cur[s]))
            heat_total = heat[0] * rates[0]
            for r in range(1, reactions):
                heat_total = heat_total + heat[r] * rates[r]
            new.append(jnp.where(active, cur[SPECIES] + stride * heat_total, cur[SPECIES]))
            cur = new
        for s in range(rows):
            o_ref[s, x] = (cur[s] - start[s]) / time_step
        return carry

    lax.fori_loop(0, u_ref.shape[1], per_x, 0)


def chemistry(fields, cell_counts, log_rate, activation, heat_release):
    smem = pl.BlockSpec(memory_space=pltpu.SMEM)
    vmem = pl.BlockSpec(memory_space=pltpu.VMEM)
    return pl.pallas_call(
        chem_kernel,
        out_shape=jax.ShapeDtypeStruct(fields.shape, jnp.float32),
        in_specs=[smem, smem, smem, vmem, vmem],
        out_specs=vmem,
    )(log_rate, activation, heat_release, fields, cell_counts)


def shift_pairs(size, step):
    return [(i, (i + step) % size) for i in range(size)]


def exchange(to_lo, to_hi, axis, size):
    if size % 2:
        from_lo = lax.ppermute(to_hi, axis, shift_pairs(size, 1))
        from_hi = lax.ppermute(to_lo, axis, shift_pairs(size, -1))
        return from_lo, from_hi
    even = lax.axis_index(axis) % 2 == 0
    inner = [(i, i + 1 if i % 2 == 0 else i - 1) for i in range(size)]
    outer = [(i, (i - 1) % size if i % 2 == 0 else (i + 1) % size) for i in range(size)]
    first = lax.ppermute(jnp.where(even, to_hi, to_lo), axis, inner)
    second = lax.ppermute(jnp.where(even, to_lo, to_hi), axis, outer)
    return jnp.where(even, second, first), jnp.where(even, first, second)


def laplace_parts(s, lo, hi):
    c = s[:, lo:hi, lo:hi]
    beside = s[:, lo - 1:hi - 1, lo:hi] + s[:, lo + 1:hi + 1, lo:hi]
    beside = beside + s[:, lo:hi, lo - 1:hi - 1] + s[:, lo:hi, lo + 1:hi + 1]
    beside = beside + jnp.roll(c, 1, 3) + jnp.roll(c, -1, 3)
    return beside - 6.0 * c


def local(state, source_in, counts, diffusivity, log_rate, activation, heat_release):
    nx = lax.axis_size("gx")
    ny = lax.axis_size("gy")
    rows, cx, cy, cz = state.shape
    spread = diffusivity[:, None, None, None]
    cell_counts = jnp.broadcast_to(counts[:, :, None], (cx, cy, cz))

    to_xm = jnp.concatenate([state[:, :2], source_in[:, :1]], 1)
    to_xp = jnp.concatenate([state[:, cx - 2:], source_in[:, cx - 1:]], 1)
    from_xm, from_xp = exchange(to_xm, to_xp, "gx", nx)

    early = chemistry(state, cell_counts, log_rate, activation, heat_release)

    def zeros(a, b):
        return jnp.zeros((rows, a, b, cz), jnp.float32)

    wide = jnp.concatenate([from_xm[:, :2], state, from_xp[:, :2]], 1)
    wide_src = jnp.concatenate([from_xm[:, 2:], source_in, from_xp[:, 2:]], 1)
    to_ym = jnp.concatenate([wide[:, 1:-1, :2], wide_src[:, :, :1]], 2)
    to_yp = jnp.concatenate([wide[:, 1:-1, cy - 2:], wide_src[:, :, cy - 1:]], 2)
    from_ym, from_yp = exchange(to_ym, to_yp, "gy", ny)
    ext = jnp.concatenate(
        [
            jnp.concatenate([zeros(1, 2), wide[:, :1], zeros(1, 2)], 2),
            jnp.concatenate([from_ym[:, :, :2], wide[:, 1:-1], from_yp[:, :, :2]], 2),
            jnp.concatenate([zeros(1, 2), wide[:, -1:], zeros(1, 2)], 2),
        ],
        1,
    )
    src = jnp.concatenate([from_ym[:, :, 2:], wide_src, from_yp[:, :, 2:]], 2)
    first_ext = ext[:, 1:-1, 1:-1] + time_step * (
        spread * laplace_parts(ext, 1, cx + 3) + src
    )
    first_section = first_ext[:, 1:-1, 1:-1]
    next_state = 0.5 * state + 0.5 * (
        first_section + time_step * (spread * laplace_parts(first_ext, 1, cx + 1) + early)
    )
    late_source = chemistry(first_section, cell_counts, log_rate, activation, heat_release)
    return (next_state, late_source)


def solution(mesh):
    in_specs = (
        P(None, "gx", "gy", None),
        P(None, "gx", "gy", None),
        P("gx", "gy"),
        P(),
        P(),
        P(),
        P(),
    )
    out_specs = (P(None, "gx", "gy", None), P(None, "gx", "gy", None))
    return jax.shard_map(local, mesh=mesh, in_specs=in_specs, out_specs=out_specs, check_vma=False)
```

```python
import jax
import jax.numpy as jnp
import numpy as np
from jax import lax
from jax.experimental import pallas as pl
from jax.experimental.pallas import tpu as pltpu
from jax.sharding import PartitionSpec as P

time_step = 0.15
reaction_table = (
    (3, 1, (4, 5)),
    (4, 0, (3, 5)),
    (5, 0, (3, 2)),
    (5, 5, (4, 2)),
    (3, 3, (0,)),
    (3, 5, (2,)),
    (4, 4, (1,)),
    (3, 4, (5,)),
    (3, 1, (6,)),
    (6, 3, (0, 1)),
    (6, 3, (5, 5)),
    (6, 4, (1, 5)),
    (6, 5, (2, 1)),
    (6, 6, (7, 1)),
    (7, 9, (5, 5)),
    (7, 3, (2, 5)),
    (7, 3, (6, 0)),
    (7, 4, (5, 6)),
    (7, 5, (6, 2)),
    (0, 9, (3, 3)),
    (2, 9, (3, 5)),
)
SPECIES = 9
CMAX = 8


def stoichiometry():
    change = np.zeros((SPECIES, len(reaction_table)), np.int64)
    for reaction, entry in enumerate(reaction_table):
        change[entry[0], reaction] -= 1
        if entry[1] < SPECIES:
            change[entry[1], reaction] -= 1
        for product in entry[2]:
            change[product, reaction] += 1
    return change


def react(start, cnt, rate_ref, act_ref, heat_ref):
    change = stoichiometry()
    reactions = len(reaction_table)
    temper = start[SPECIES]
    coeffs = [jnp.exp(rate_ref[r] - act_ref[r] / temper) for r in range(reactions)]
    heat = [heat_ref[r] for r in range(reactions)]
    stride = time_step / cnt.astype(jnp.float32)
    cur = list(start)
    for turn in range(CMAX):
        active = turn < cnt
        rates = []
        for r, entry in enumerate(reaction_table):
            term = coeffs[r] * cur[entry[0]]
            if entry[1] < SPECIES:
                term = term * cur[entry[1]]
            rates.append(term)
        new = []
        for s in range(SPECIES):
            total = None
            for r in range(reactions):
                c = int(change[s, r])
                if c == 0:
                    continue
                piece = rates[r] if abs(c) == 1 else rates[r] * float(abs(c))
                if total is None:
                    total = piece if c > 0 else -piece
                elif c > 0:
                    total = total + piece
                else:
                    total = total - piece
            if total is None:
                new.append(cur[s])
            else:
                new.append(jnp.where(active, cur[s] + stride * total, cur[s]))
        heat_total = heat[0] * rates[0]
        for r in range(1, reactions):
            heat_total = heat_total + heat[r] * rates[r]
        new.append(jnp.where(active, cur[SPECIES] + stride * heat_total, cur[SPECIES]))
        cur = new
    return [(cur[s] - start[s]) / time_step for s in range(len(start))]


def chem_kernel(rate_ref, act_ref, heat_ref, u_ref, cnt_ref, o_ref):
    rows = u_ref.shape[0]

    def per_x(x, carry):
        start = [u_ref[s, x] for s in range(rows)]
        out = react(start, cnt_ref[x], rate_ref, act_ref, heat_ref)
        for s in range(rows):
            o_ref[s, x] = out[s]
        return carry

    lax.fori_loop(0, u_ref.shape[1], per_x, 0)


def finish_kernel(
    diff_ref, rate_ref, act_ref, heat_ref, ext_ref, src_ref, early_ref, cnt_ref,
    next_ref, late_ref, first_ref,
):
    rows, cx, cy, _ = early_ref.shape
    lanes = ext_ref.shape[3]

    def laplace(centre, xm, xp, ym, yp):
        beside = xm + xp
        beside = beside + ym + yp
        beside = beside + pltpu.roll(centre, 1, 1) + pltpu.roll(centre, lanes - 1, 1)
        return beside - 6.0 * centre

    def first_row(i, carry):
        e = i + 1
        for r in range(rows):
            for lo in (0, 2):
                centre = ext_ref[r, e, pl.ds(lo + 1, cy)]
                lap = laplace(
                    centre,
                    ext_ref[r, e - 1, pl.ds(lo + 1, cy)],
                    ext_ref[r, e + 1, pl.ds(lo + 1, cy)],
                    ext_ref[r, e, pl.ds(lo, cy)],
                    ext_ref[r, e, pl.ds(lo + 2, cy)],
                )
                first_ref[r, i, pl.ds(lo, cy)] = centre + time_step * (
                    diff_ref[r] * lap + src_ref[r, i, pl.ds(lo, cy)]
                )
        return carry

    lax.fori_loop(0, cx + 2, first_row, 0)

    def box_row(x, carry):
        start = []
        for r in range(rows):
            centre = first_ref[r, x + 1, pl.ds(1, cy)]
            lap = laplace(
                centre,
                first_ref[r, x, pl.ds(1, cy)],
                first_ref[r, x + 2, pl.ds(1, cy)],
                first_ref[r, x + 1, pl.ds(0, cy)],
                first_ref[r, x + 1, pl.ds(2, cy)],
            )
            state = ext_ref[r, x + 2, pl.ds(2, cy)]
            next_ref[r, x] = 0.5 * state + 0.5 * (
                centre + time_step * (diff_ref[r] * lap + early_ref[r, x])
            )
            start.append(centre)
        out = react(start, cnt_ref[x], rate_ref, act_ref, heat_ref)
        for r in range(rows):
            late_ref[r, x] = out[r]
        return carry

    lax.fori_loop(0, cx, box_row, 0)


def finish(ext, src, early, cell_counts, diffusivity, log_rate, activation, heat_release):
    rows, cx, cy, cz = early.shape
    smem = pl.BlockSpec(memory_space=pltpu.SMEM)
    vmem = pl.BlockSpec(memory_space=pltpu.VMEM)
    box = jax.ShapeDtypeStruct(early.shape, jnp.float32)
    return pl.pallas_call(
        finish_kernel,
        out_shape=(box, box),
        in_specs=[smem, smem, smem, smem, vmem, vmem, vmem, vmem],
        out_specs=(vmem, vmem),
        scratch_shapes=[pltpu.VMEM((rows, cx + 2, 2 * cy, cz), jnp.float32)],
    )(diffusivity, log_rate, activation, heat_release, ext, src, early, cell_counts)


def chemistry(fields, cell_counts, log_rate, activation, heat_release):
    smem = pl.BlockSpec(memory_space=pltpu.SMEM)
    vmem = pl.BlockSpec(memory_space=pltpu.VMEM)
    return pl.pallas_call(
        chem_kernel,
        out_shape=jax.ShapeDtypeStruct(fields.shape, jnp.float32),
        in_specs=[smem, smem, smem, vmem, vmem],
        out_specs=vmem,
    )(log_rate, activation, heat_release, fields, cell_counts)


def shift_pairs(size, step):
    return [(i, (i + step) % size) for i in range(size)]


def exchange(to_lo, to_hi, axis, size):
    if size % 2:
        from_lo = lax.ppermute(to_hi, axis, shift_pairs(size, 1))
        from_hi = lax.ppermute(to_lo, axis, shift_pairs(size, -1))
        return from_lo, from_hi
    even = lax.axis_index(axis) % 2 == 0
    inner = [(i, i + 1 if i % 2 == 0 else i - 1) for i in range(size)]
    outer = [(i, (i - 1) % size if i % 2 == 0 else (i + 1) % size) for i in range(size)]
    first = lax.ppermute(jnp.where(even, to_hi, to_lo), axis, inner)
    second = lax.ppermute(jnp.where(even, to_lo, to_hi), axis, outer)
    return jnp.where(even, second, first), jnp.where(even, first, second)


def local(state, source_in, counts, diffusivity, log_rate, activation, heat_release):
    nx = lax.axis_size("gx")
    ny = lax.axis_size("gy")
    rows, cx, cy, cz = state.shape
    cell_counts = jnp.broadcast_to(counts[:, :, None], (cx, cy, cz))

    to_xm = jnp.concatenate([state[:, :2], source_in[:, :1]], 1)
    to_xp = jnp.concatenate([state[:, cx - 2:], source_in[:, cx - 1:]], 1)
    from_xm, from_xp = exchange(to_xm, to_xp, "gx", nx)

    early = chemistry(state, cell_counts, log_rate, activation, heat_release)

    def zeros(a, b):
        return jnp.zeros((rows, a, b, cz), jnp.float32)

    wide = jnp.concatenate([from_xm[:, :2], state, from_xp[:, :2]], 1)
    wide_src = jnp.concatenate([from_xm[:, 2:], source_in, from_xp[:, 2:]], 1)
    to_ym = jnp.concatenate([wide[:, 1:-1, :2], wide_src[:, :, :1]], 2)
    to_yp = jnp.concatenate([wide[:, 1:-1, cy - 2:], wide_src[:, :, cy - 1:]], 2)
    from_ym, from_yp = exchange(to_ym, to_yp, "gy", ny)
    ext = jnp.concatenate(
        [
            jnp.concatenate([zeros(1, 2), wide[:, :1], zeros(1, 2)], 2),
            jnp.concatenate([from_ym[:, :, :2], wide[:, 1:-1], from_yp[:, :, :2]], 2),
            jnp.concatenate([zeros(1, 2), wide[:, -1:], zeros(1, 2)], 2),
        ],
        1,
    )
    src = jnp.concatenate([from_ym[:, :, 2:], wide_src, from_yp[:, :, 2:]], 2)
    next_state, late_source = finish(
        ext, src, early, cell_counts, diffusivity, log_rate, activation, heat_release
    )
    return (next_state, late_source)


def solution(mesh):
    in_specs = (
        P(None, "gx", "gy", None),
        P(None, "gx", "gy", None),
        P("gx", "gy"),
        P(),
        P(),
        P(),
        P(),
    )
    out_specs = (P(None, "gx", "gy", None), P(None, "gx", "gy", None))
    return jax.shard_map(local, mesh=mesh, in_specs=in_specs, out_specs=out_specs, check_vma=False)
```

```python
import jax
import jax.numpy as jnp
import numpy as np
from jax import lax
from jax.experimental import pallas as pl
from jax.experimental.pallas import tpu as pltpu
from jax.sharding import PartitionSpec as P

time_step = 0.15
reaction_table = (
    (3, 1, (4, 5)),
    (4, 0, (3, 5)),
    (5, 0, (3, 2)),
    (5, 5, (4, 2)),
    (3, 3, (0,)),
    (3, 5, (2,)),
    (4, 4, (1,)),
    (3, 4, (5,)),
    (3, 1, (6,)),
    (6, 3, (0, 1)),
    (6, 3, (5, 5)),
    (6, 4, (1, 5)),
    (6, 5, (2, 1)),
    (6, 6, (7, 1)),
    (7, 9, (5, 5)),
    (7, 3, (2, 5)),
    (7, 3, (6, 0)),
    (7, 4, (5, 6)),
    (7, 5, (6, 2)),
    (0, 9, (3, 3)),
    (2, 9, (3, 5)),
)
SPECIES = 9
CMAX = 8


def stoichiometry():
    change = np.zeros((SPECIES, len(reaction_table)), np.int64)
    for reaction, entry in enumerate(reaction_table):
        change[entry[0], reaction] -= 1
        if entry[1] < SPECIES:
            change[entry[1], reaction] -= 1
        for product in entry[2]:
            change[product, reaction] += 1
    return change


def react(start, cnt, rate_ref, act_ref, heat_ref):
    change = stoichiometry()
    reactions = len(reaction_table)
    temper = start[SPECIES]
    coeffs = [jnp.exp(rate_ref[r] - act_ref[r] / temper) for r in range(reactions)]
    heat = [heat_ref[r] for r in range(reactions)]
    stride = time_step / cnt.astype(jnp.float32)
    cur = list(start)
    for turn in range(CMAX):
        active = turn < cnt
        rates = []
        for r, entry in enumerate(reaction_table):
            term = coeffs[r] * cur[entry[0]]
            if entry[1] < SPECIES:
                term = term * cur[entry[1]]
            rates.append(term)
        new = []
        for s in range(SPECIES):
            total = None
            for r in range(reactions):
                c = int(change[s, r])
                if c == 0:
                    continue
                piece = rates[r] if abs(c) == 1 else rates[r] * float(abs(c))
                if total is None:
                    total = piece if c > 0 else -piece
                elif c > 0:
                    total = total + piece
                else:
                    total = total - piece
            if total is None:
                new.append(cur[s])
            else:
                new.append(jnp.where(active, cur[s] + stride * total, cur[s]))
        heat_total = heat[0] * rates[0]
        for r in range(1, reactions):
            heat_total = heat_total + heat[r] * rates[r]
        new.append(jnp.where(active, cur[SPECIES] + stride * heat_total, cur[SPECIES]))
        cur = new
    return [(cur[s] - start[s]) / time_step for s in range(len(start))]


def chem_kernel(rate_ref, act_ref, heat_ref, u_ref, cnt_ref, o_ref):
    rows = u_ref.shape[0]

    def per_x(x, carry):
        start = [u_ref[s, x] for s in range(rows)]
        out = react(start, cnt_ref[x], rate_ref, act_ref, heat_ref)
        for s in range(rows):
            o_ref[s, x] = out[s]
        return carry

    lax.fori_loop(0, u_ref.shape[1], per_x, 0)


def finish_kernel(
    diff_ref, rate_ref, act_ref, heat_ref, ext_ref, src_ref, early_ref, cnt_ref,
    next_ref, late_ref, first_ref,
):
    rows, cx, cy, _ = early_ref.shape
    lanes = ext_ref.shape[3]

    def laplace(centre, xm, xp, ym, yp):
        beside = xm + xp
        beside = beside + ym + yp
        beside = beside + pltpu.roll(centre, 1, 1) + pltpu.roll(centre, lanes - 1, 1)
        return beside - 6.0 * centre

    def first_row(i, carry):
        e = i + 1
        for r in range(rows):
            for lo in (0, 2):
                centre = ext_ref[r, e, pl.ds(lo + 1, cy)]
                lap = laplace(
                    centre,
                    ext_ref[r, e - 1, pl.ds(lo + 1, cy)],
                    ext_ref[r, e + 1, pl.ds(lo + 1, cy)],
                    ext_ref[r, e, pl.ds(lo, cy)],
                    ext_ref[r, e, pl.ds(lo + 2, cy)],
                )
                first_ref[r, i, pl.ds(lo, cy)] = centre + time_step * (
                    diff_ref[r] * lap + src_ref[r, i, pl.ds(lo, cy)]
                )
        return carry

    lax.fori_loop(0, cx + 2, first_row, 0)

    def box_row(x, carry):
        start = []
        for r in range(rows):
            centre = first_ref[r, x + 1, pl.ds(1, cy)]
            lap = laplace(
                centre,
                first_ref[r, x, pl.ds(1, cy)],
                first_ref[r, x + 2, pl.ds(1, cy)],
                first_ref[r, x + 1, pl.ds(0, cy)],
                first_ref[r, x + 1, pl.ds(2, cy)],
            )
            state = ext_ref[r, x + 2, pl.ds(2, cy)]
            next_ref[r, x] = 0.5 * state + 0.5 * (
                centre + time_step * (diff_ref[r] * lap + early_ref[r, x])
            )
            start.append(centre)
        out = react(start, cnt_ref[x], rate_ref, act_ref, heat_ref)
        for r in range(rows):
            late_ref[r, x] = out[r]
        return carry

    lax.fori_loop(0, cx, box_row, 0)


def finish(ext, src, early, cell_counts, diffusivity, log_rate, activation, heat_release):
    rows, cx, cy, cz = early.shape
    smem = pl.BlockSpec(memory_space=pltpu.SMEM)
    vmem = pl.BlockSpec(memory_space=pltpu.VMEM)
    box = jax.ShapeDtypeStruct(early.shape, jnp.float32)
    return pl.pallas_call(
        finish_kernel,
        out_shape=(box, box),
        in_specs=[smem, smem, smem, smem, vmem, vmem, vmem, vmem],
        out_specs=(vmem, vmem),
        scratch_shapes=[pltpu.VMEM((rows, cx + 2, 2 * cy, cz), jnp.float32)],
    )(diffusivity, log_rate, activation, heat_release, ext, src, early, cell_counts)


def chemistry(fields, cell_counts, log_rate, activation, heat_release):
    smem = pl.BlockSpec(memory_space=pltpu.SMEM)
    vmem = pl.BlockSpec(memory_space=pltpu.VMEM)
    return pl.pallas_call(
        chem_kernel,
        out_shape=jax.ShapeDtypeStruct(fields.shape, jnp.float32),
        in_specs=[smem, smem, smem, vmem, vmem],
        out_specs=vmem,
    )(log_rate, activation, heat_release, fields, cell_counts)


def shift_pairs(size, step):
    return [(i, (i + step) % size) for i in range(size)]


def exchange(to_lo, to_hi, axis, size):
    if size % 2:
        from_lo = lax.ppermute(to_hi, axis, shift_pairs(size, 1))
        from_hi = lax.ppermute(to_lo, axis, shift_pairs(size, -1))
        return from_lo, from_hi
    even = lax.axis_index(axis) % 2 == 0
    inner = [(i, i + 1 if i % 2 == 0 else i - 1) for i in range(size)]
    outer = [(i, (i - 1) % size if i % 2 == 0 else (i + 1) % size) for i in range(size)]
    first = lax.ppermute(jnp.where(even, to_hi, to_lo), axis, inner)
    second = lax.ppermute(jnp.where(even, to_lo, to_hi), axis, outer)
    return jnp.where(even, second, first), jnp.where(even, first, second)


def local(state, source_in, counts, diffusivity, log_rate, activation, heat_release):
    nx = lax.axis_size("gx")
    ny = lax.axis_size("gy")
    rows, cx, cy, cz = state.shape
    cell_counts = jnp.broadcast_to(counts[:, :, None], (cx, cy, cz))

    to_xm = jnp.concatenate([state[:, :2], source_in[:, :1]], 1)
    to_xp = jnp.concatenate([state[:, cx - 2:], source_in[:, cx - 1:]], 1)
    from_xm, from_xp = exchange(to_xm, to_xp, "gx", nx)

    early = chemistry(state, cell_counts, log_rate, activation, heat_release)
    early, from_xm, from_xp = lax.optimization_barrier((early, from_xm, from_xp))

    def zeros(a, b):
        return jnp.zeros((rows, a, b, cz), jnp.float32)

    wide = jnp.concatenate([from_xm[:, :2], state, from_xp[:, :2]], 1)
    wide_src = jnp.concatenate([from_xm[:, 2:], source_in, from_xp[:, 2:]], 1)
    to_ym = jnp.concatenate([wide[:, 1:-1, :2], wide_src[:, :, :1]], 2)
    to_yp = jnp.concatenate([wide[:, 1:-1, cy - 2:], wide_src[:, :, cy - 1:]], 2)
    from_ym, from_yp = exchange(to_ym, to_yp, "gy", ny)
    ext = jnp.concatenate(
        [
            jnp.concatenate([zeros(1, 2), wide[:, :1], zeros(1, 2)], 2),
            jnp.concatenate([from_ym[:, :, :2], wide[:, 1:-1], from_yp[:, :, :2]], 2),
            jnp.concatenate([zeros(1, 2), wide[:, -1:], zeros(1, 2)], 2),
        ],
        1,
    )
    src = jnp.concatenate([from_ym[:, :, 2:], wide_src, from_yp[:, :, 2:]], 2)
    next_state, late_source = finish(
        ext, src, early, cell_counts, diffusivity, log_rate, activation, heat_release
    )
    return (next_state, late_source)


def solution(mesh):
    in_specs = (
        P(None, "gx", "gy", None),
        P(None, "gx", "gy", None),
        P("gx", "gy"),
        P(),
        P(),
        P(),
        P(),
    )
    out_specs = (P(None, "gx", "gy", None), P(None, "gx", "gy", None))
    return jax.shard_map(local, mesh=mesh, in_specs=in_specs, out_specs=out_specs, check_vma=False)
```

```python
import jax
import jax.numpy as jnp
import numpy as np
from jax import lax
from jax.experimental import pallas as pl
from jax.experimental.pallas import tpu as pltpu
from jax.sharding import PartitionSpec as P

time_step = 0.15
reaction_table = (
    (3, 1, (4, 5)),
    (4, 0, (3, 5)),
    (5, 0, (3, 2)),
    (5, 5, (4, 2)),
    (3, 3, (0,)),
    (3, 5, (2,)),
    (4, 4, (1,)),
    (3, 4, (5,)),
    (3, 1, (6,)),
    (6, 3, (0, 1)),
    (6, 3, (5, 5)),
    (6, 4, (1, 5)),
    (6, 5, (2, 1)),
    (6, 6, (7, 1)),
    (7, 9, (5, 5)),
    (7, 3, (2, 5)),
    (7, 3, (6, 0)),
    (7, 4, (5, 6)),
    (7, 5, (6, 2)),
    (0, 9, (3, 3)),
    (2, 9, (3, 5)),
)
SPECIES = 9
CMAX = 8


def stoichiometry():
    change = np.zeros((SPECIES, len(reaction_table)), np.int64)
    for reaction, entry in enumerate(reaction_table):
        change[entry[0], reaction] -= 1
        if entry[1] < SPECIES:
            change[entry[1], reaction] -= 1
        for product in entry[2]:
            change[product, reaction] += 1
    return change


def react(start, cnt, rate_ref, act_ref, heat_ref):
    change = stoichiometry()
    reactions = len(reaction_table)
    temper = start[SPECIES]
    coeffs = [jnp.exp(rate_ref[r] - act_ref[r] / temper) for r in range(reactions)]
    heat = [heat_ref[r] for r in range(reactions)]
    stride = time_step / cnt.astype(jnp.float32)
    cur = list(start)
    for turn in range(CMAX):
        active = turn < cnt
        rates = []
        for r, entry in enumerate(reaction_table):
            term = coeffs[r] * cur[entry[0]]
            if entry[1] < SPECIES:
                term = term * cur[entry[1]]
            rates.append(term)
        new = []
        for s in range(SPECIES):
            total = None
            for r in range(reactions):
                c = int(change[s, r])
                if c == 0:
                    continue
                piece = rates[r] if abs(c) == 1 else rates[r] * float(abs(c))
                if total is None:
                    total = piece if c > 0 else -piece
                elif c > 0:
                    total = total + piece
                else:
                    total = total - piece
            if total is None:
                new.append(cur[s])
            else:
                new.append(jnp.where(active, cur[s] + stride * total, cur[s]))
        heat_total = heat[0] * rates[0]
        for r in range(1, reactions):
            heat_total = heat_total + heat[r] * rates[r]
        new.append(jnp.where(active, cur[SPECIES] + stride * heat_total, cur[SPECIES]))
        cur = new
    return [(cur[s] - start[s]) / time_step for s in range(len(start))]


def chem_kernel(rate_ref, act_ref, heat_ref, u_ref, cnt_ref, o_ref):
    rows = u_ref.shape[0]

    def per_x(x, carry):
        start = [u_ref[s, x] for s in range(rows)]
        out = react(start, cnt_ref[x], rate_ref, act_ref, heat_ref)
        for s in range(rows):
            o_ref[s, x] = out[s]
        return carry

    lax.fori_loop(0, u_ref.shape[1], per_x, 0)


def laplace_tile(centre, xm, xp, ym, yp):
    lanes = centre.shape[-1]
    beside = xm + xp
    beside = beside + ym + yp
    beside = beside + pltpu.roll(centre, 1, 1) + pltpu.roll(centre, lanes - 1, 1)
    return beside - 6.0 * centre


def first_rows(diff_ref, box_ref, src_ref, first_ref, e_of, s_of, rows_i, cy):
    rows = first_ref.shape[0]
    for i in rows_i:
        e, s = e_of(i), s_of(i)
        for r in range(rows):
            for lo in (0, 2):
                centre = box_ref[r, e, pl.ds(lo + 1, cy)]
                lap = laplace_tile(
                    centre,
                    box_ref[r, e - 1, pl.ds(lo + 1, cy)],
                    box_ref[r, e + 1, pl.ds(lo + 1, cy)],
                    box_ref[r, e, pl.ds(lo, cy)],
                    box_ref[r, e, pl.ds(lo + 2, cy)],
                )
                first_ref[r, i, pl.ds(lo, cy)] = centre + time_step * (
                    diff_ref[r] * lap + src_ref[r, s, pl.ds(lo, cy)]
                )


def partial_kernel(
    diff_ref, rate_ref, act_ref, heat_ref, wide_ref, wsrc_ref, cnt_ref, first_ref, late_ref
):
    rows, cx = wide_ref.shape[0], wide_ref.shape[1]
    cy = late_ref.shape[2]
    first_rows(
        diff_ref, wide_ref, wsrc_ref, first_ref,
        lambda i: i - 1, lambda i: i - 1, range(2, cx), cy,
    )

    def per_x(x, carry):
        start = [first_ref[r, x + 1, pl.ds(1, cy)] for r in range(rows)]
        out = react(start, cnt_ref[x], rate_ref, act_ref, heat_ref)
        for r in range(rows):
            late_ref[r, x] = out[r]
        return carry

    lax.fori_loop(1, cx - 1, per_x, 0)


def finish_kernel(
    diff_ref, rate_ref, act_ref, heat_ref, ext_ref, src_ref, early_ref, cnt_ref,
    part_ref, late_part_ref, next_ref, late_ref, first_ref,
):
    rows, cx, cy, _ = early_ref.shape
    edge = (0, 1, cx, cx + 1)
    first_rows(
        diff_ref, ext_ref, src_ref, first_ref,
        lambda i: i + 1, lambda i: i, edge, cy,
    )
    for i in range(2, cx):
        for r in range(rows):
            first_ref[r, i] = part_ref[r, i]

    for x in range(cx):
        start = []
        for r in range(rows):
            centre = first_ref[r, x + 1, pl.ds(1, cy)]
            lap = laplace_tile(
                centre,
                first_ref[r, x, pl.ds(1, cy)],
                first_ref[r, x + 2, pl.ds(1, cy)],
                first_ref[r, x + 1, pl.ds(0, cy)],
                first_ref[r, x + 1, pl.ds(2, cy)],
            )
            state = ext_ref[r, x + 2, pl.ds(2, cy)]
            next_ref[r, x] = 0.5 * state + 0.5 * (
                centre + time_step * (diff_ref[r] * lap + early_ref[r, x])
            )
            start.append(centre)
        if x in (0, cx - 1):
            out = react(start, cnt_ref[x], rate_ref, act_ref, heat_ref)
            for r in range(rows):
                late_ref[r, x] = out[r]
        else:
            for r in range(rows):
                late_ref[r, x] = late_part_ref[r, x]


def partial(wide, wide_src, cell_counts, diffusivity, log_rate, activation, heat_release):
    rows, cx, _, cz = wide.shape
    cy = cell_counts.shape[1]
    smem = pl.BlockSpec(memory_space=pltpu.SMEM)
    vmem = pl.BlockSpec(memory_space=pltpu.VMEM)
    return pl.pallas_call(
        partial_kernel,
        out_shape=(
            jax.ShapeDtypeStruct((rows, cx + 2, 2 * cy, cz), jnp.float32),
            jax.ShapeDtypeStruct((rows, cx, cy, cz), jnp.float32),
        ),
        in_specs=[smem, smem, smem, smem, vmem, vmem, vmem],
        out_specs=(vmem, vmem),
    )(diffusivity, log_rate, activation, heat_release, wide, wide_src, cell_counts)


def finish(ext, src, early, cell_counts, part, late_part, diffusivity, log_rate, activation, heat_release):
    rows, cx, cy, cz = early.shape
    smem = pl.BlockSpec(memory_space=pltpu.SMEM)
    vmem = pl.BlockSpec(memory_space=pltpu.VMEM)
    box = jax.ShapeDtypeStruct(early.shape, jnp.float32)
    return pl.pallas_call(
        finish_kernel,
        out_shape=(box, box),
        in_specs=[smem, smem, smem, smem] + [vmem] * 6,
        out_specs=(vmem, vmem),
        scratch_shapes=[pltpu.VMEM((rows, cx + 2, 2 * cy, cz), jnp.float32)],
    )(diffusivity, log_rate, activation, heat_release, ext, src, early, cell_counts, part, late_part)


def chemistry(fields, cell_counts, log_rate, activation, heat_release):
    smem = pl.BlockSpec(memory_space=pltpu.SMEM)
    vmem = pl.BlockSpec(memory_space=pltpu.VMEM)
    return pl.pallas_call(
        chem_kernel,
        out_shape=jax.ShapeDtypeStruct(fields.shape, jnp.float32),
        in_specs=[smem, smem, smem, vmem, vmem],
        out_specs=vmem,
    )(log_rate, activation, heat_release, fields, cell_counts)


def shift_pairs(size, step):
    return [(i, (i + step) % size) for i in range(size)]


def exchange(to_lo, to_hi, axis, size):
    if size % 2:
        from_lo = lax.ppermute(to_hi, axis, shift_pairs(size, 1))
        from_hi = lax.ppermute(to_lo, axis, shift_pairs(size, -1))
        return from_lo, from_hi
    even = lax.axis_index(axis) % 2 == 0
    inner = [(i, i + 1 if i % 2 == 0 else i - 1) for i in range(size)]
    outer = [(i, (i - 1) % size if i % 2 == 0 else (i + 1) % size) for i in range(size)]
    first = lax.ppermute(jnp.where(even, to_hi, to_lo), axis, inner)
    second = lax.ppermute(jnp.where(even, to_lo, to_hi), axis, outer)
    return jnp.where(even, second, first), jnp.where(even, first, second)


def local(state, source_in, counts, diffusivity, log_rate, activation, heat_release):
    nx = lax.axis_size("gx")
    ny = lax.axis_size("gy")
    rows, cx, cy, cz = state.shape
    cell_counts = jnp.broadcast_to(counts[:, :, None], (cx, cy, cz))

    def zeros(a, b):
        return jnp.zeros((rows, a, b, cz), jnp.float32)

    to_ym = jnp.concatenate([state[:, :, :2], source_in[:, :, :1]], 2)
    to_yp = jnp.concatenate([state[:, :, cy - 2:], source_in[:, :, cy - 1:]], 2)
    from_ym, from_yp = exchange(to_ym, to_yp, "gy", ny)
    wide = jnp.concatenate([from_ym[:, :, :2], state, from_yp[:, :, :2]], 2)
    wide_src = jnp.concatenate([from_ym[:, :, 2:], source_in, from_yp[:, :, 2:]], 2)

    def corners(x):
        return jnp.concatenate([wide[:, x:x + 1, 1:2], wide[:, x:x + 1, cy + 2:cy + 3], zeros(1, cy - 2)], 2)

    to_xm = jnp.concatenate([state[:, :2], source_in[:, :1], corners(0)], 1)
    to_xp = jnp.concatenate([state[:, cx - 2:], source_in[:, cx - 1:], corners(cx - 1)], 1)
    from_xm, from_xp = exchange(to_xm, to_xp, "gx", nx)

    early = chemistry(state, cell_counts, log_rate, activation, heat_release)
    part, late_part = partial(
        wide, wide_src, cell_counts, diffusivity, log_rate, activation, heat_release
    )
    part, late_part, from_xm, from_xp = lax.optimization_barrier(
        (part, late_part, from_xm, from_xp)
    )

    def edge_row(got, k):
        return jnp.concatenate([zeros(1, 1), got[:, 3:, :1], got[:, k:k + 1], got[:, 3:, 1:2], zeros(1, 1)], 2)

    ext = jnp.concatenate(
        [
            jnp.concatenate([zeros(1, 2), from_xm[:, :1], zeros(1, 2)], 2),
            edge_row(from_xm, 1),
            wide,
            edge_row(from_xp, 0),
            jnp.concatenate([zeros(1, 2), from_xp[:, 1:2], zeros(1, 2)], 2),
        ],
        1,
    )
    src = jnp.concatenate(
        [
            jnp.concatenate([zeros(1, 1), from_xm[:, 2:3], zeros(1, 1)], 2),
            wide_src,
            jnp.concatenate([zeros(1, 1), from_xp[:, 2:3], zeros(1, 1)], 2),
        ],
        1,
    )
    next_state, late_source = finish(
        ext, src, early, cell_counts, part, late_part,
        diffusivity, log_rate, activation, heat_release,
    )
    return (next_state, late_source)


def solution(mesh):
    in_specs = (
        P(None, "gx", "gy", None),
        P(None, "gx", "gy", None),
        P("gx", "gy"),
        P(),
        P(),
        P(),
        P(),
    )
    out_specs = (P(None, "gx", "gy", None), P(None, "gx", "gy", None))
    return jax.shard_map(local, mesh=mesh, in_specs=in_specs, out_specs=out_specs, check_vma=False)
```

```python
import jax
import jax.numpy as jnp
import numpy as np
from jax import lax
from jax.experimental import pallas as pl
from jax.experimental.pallas import tpu as pltpu
from jax.sharding import PartitionSpec as P

time_step = 0.15
reaction_table = (
    (3, 1, (4, 5)),
    (4, 0, (3, 5)),
    (5, 0, (3, 2)),
    (5, 5, (4, 2)),
    (3, 3, (0,)),
    (3, 5, (2,)),
    (4, 4, (1,)),
    (3, 4, (5,)),
    (3, 1, (6,)),
    (6, 3, (0, 1)),
    (6, 3, (5, 5)),
    (6, 4, (1, 5)),
    (6, 5, (2, 1)),
    (6, 6, (7, 1)),
    (7, 9, (5, 5)),
    (7, 3, (2, 5)),
    (7, 3, (6, 0)),
    (7, 4, (5, 6)),
    (7, 5, (6, 2)),
    (0, 9, (3, 3)),
    (2, 9, (3, 5)),
)
SPECIES = 9
CMAX = 8


def stoichiometry():
    change = np.zeros((SPECIES, len(reaction_table)), np.int64)
    for reaction, entry in enumerate(reaction_table):
        change[entry[0], reaction] -= 1
        if entry[1] < SPECIES:
            change[entry[1], reaction] -= 1
        for product in entry[2]:
            change[product, reaction] += 1
    return change


def react(start, cnt, rate_ref, act_ref, heat_ref):
    change = stoichiometry()
    reactions = len(reaction_table)
    temper = start[SPECIES]
    coeffs = [jnp.exp(rate_ref[r] - act_ref[r] / temper) for r in range(reactions)]
    heat = [heat_ref[r] for r in range(reactions)]
    stride = time_step / cnt.astype(jnp.float32)
    cur = list(start)
    for turn in range(CMAX):
        step = jnp.where(turn < cnt, stride, 0.0)
        rates = []
        for r, entry in enumerate(reaction_table):
            term = coeffs[r] * cur[entry[0]]
            if entry[1] < SPECIES:
                term = term * cur[entry[1]]
            rates.append(term)
        new = []
        for s in range(SPECIES):
            total = None
            for r in range(reactions):
                c = int(change[s, r])
                if c == 0:
                    continue
                piece = rates[r] if abs(c) == 1 else rates[r] * float(abs(c))
                if total is None:
                    total = piece if c > 0 else -piece
                elif c > 0:
                    total = total + piece
                else:
                    total = total - piece
            if total is None:
                new.append(cur[s])
            else:
                new.append(cur[s] + step * total)
        heat_total = heat[0] * rates[0]
        for r in range(1, reactions):
            heat_total = heat_total + heat[r] * rates[r]
        new.append(cur[SPECIES] + step * heat_total)
        cur = new
    return [(cur[s] - start[s]) / time_step for s in range(len(start))]


def chem_kernel(rate_ref, act_ref, heat_ref, u_ref, cnt_ref, o_ref):
    rows = u_ref.shape[0]

    def per_x(x, carry):
        start = [u_ref[s, x] for s in range(rows)]
        out = react(start, cnt_ref[x], rate_ref, act_ref, heat_ref)
        for s in range(rows):
            o_ref[s, x] = out[s]
        return carry

    lax.fori_loop(0, u_ref.shape[1], per_x, 0)


def finish_kernel(
    diff_ref, rate_ref, act_ref, heat_ref, wide_ref, wsrc_ref, ym_ref, yp_ref,
    early_ref, cnt_ref, next_ref, late_ref, ext_ref, src_ref, first_ref,
):
    rows, cx, cy, _ = early_ref.shape
    lanes = ext_ref.shape[3]
    ext_ref[...] = jnp.zeros(ext_ref.shape, jnp.float32)
    src_ref[...] = jnp.zeros(src_ref.shape, jnp.float32)
    for r in range(rows):
        for e in range(cx + 4):
            ext_ref[r, e, pl.ds(2, cy)] = wide_ref[r, e]
        for i in range(cx + 2):
            ext_ref[r, i + 1, pl.ds(0, 2)] = ym_ref[r, i, pl.ds(0, 2)]
            ext_ref[r, i + 1, pl.ds(cy + 2, 2)] = yp_ref[r, i, pl.ds(0, 2)]
            src_ref[r, i, pl.ds(1, cy)] = wsrc_ref[r, i]
            src_ref[r, i, pl.ds(0, 1)] = ym_ref[r, i, pl.ds(2, 1)]
            src_ref[r, i, pl.ds(cy + 1, 1)] = yp_ref[r, i, pl.ds(2, 1)]

    def laplace(centre, xm, xp, ym, yp):
        beside = xm + xp
        beside = beside + ym + yp
        beside = beside + pltpu.roll(centre, 1, 1) + pltpu.roll(centre, lanes - 1, 1)
        return beside - 6.0 * centre

    def first_row(i, carry):
        e = i + 1
        for r in range(rows):
            for lo in (0, 2):
                centre = ext_ref[r, e, pl.ds(lo + 1, cy)]
                lap = laplace(
                    centre,
                    ext_ref[r, e - 1, pl.ds(lo + 1, cy)],
                    ext_ref[r, e + 1, pl.ds(lo + 1, cy)],
                    ext_ref[r, e, pl.ds(lo, cy)],
                    ext_ref[r, e, pl.ds(lo + 2, cy)],
                )
                first_ref[r, i, pl.ds(lo, cy)] = centre + time_step * (
                    diff_ref[r] * lap + src_ref[r, i, pl.ds(lo, cy)]
                )
        return carry

    lax.fori_loop(0, cx + 2, first_row, 0)

    def box_row(x, carry):
        start = []
        for r in range(rows):
            centre = first_ref[r, x + 1, pl.ds(1, cy)]
            lap = laplace(
                centre,
                first_ref[r, x, pl.ds(1, cy)],
                first_ref[r, x + 2, pl.ds(1, cy)],
                first_ref[r, x + 1, pl.ds(0, cy)],
                first_ref[r, x + 1, pl.ds(2, cy)],
            )
            state = ext_ref[r, x + 2, pl.ds(2, cy)]
            next_ref[r, x] = 0.5 * state + 0.5 * (
                centre + time_step * (diff_ref[r] * lap + early_ref[r, x])
            )
            start.append(centre)
        out = react(start, cnt_ref[x], rate_ref, act_ref, heat_ref)
        for r in range(rows):
            late_ref[r, x] = out[r]
        return carry

    lax.fori_loop(0, cx, box_row, 0)


def finish(wide, wide_src, from_ym, from_yp, early, cell_counts, diffusivity, log_rate, activation, heat_release):
    rows, cx, cy, cz = early.shape
    smem = pl.BlockSpec(memory_space=pltpu.SMEM)
    vmem = pl.BlockSpec(memory_space=pltpu.VMEM)
    box = jax.ShapeDtypeStruct(early.shape, jnp.float32)
    return pl.pallas_call(
        finish_kernel,
        out_shape=(box, box),
        in_specs=[smem, smem, smem, smem] + [vmem] * 6,
        out_specs=(vmem, vmem),
        scratch_shapes=[
            pltpu.VMEM((rows, cx + 4, 2 * cy, cz), jnp.float32),
            pltpu.VMEM((rows, cx + 2, 2 * cy, cz), jnp.float32),
            pltpu.VMEM((rows, cx + 2, 2 * cy, cz), jnp.float32),
        ],
    )(
        diffusivity, log_rate, activation, heat_release,
        wide, wide_src, from_ym, from_yp, early, cell_counts,
    )


def chemistry(fields, cell_counts, log_rate, activation, heat_release):
    smem = pl.BlockSpec(memory_space=pltpu.SMEM)
    vmem = pl.BlockSpec(memory_space=pltpu.VMEM)
    return pl.pallas_call(
        chem_kernel,
        out_shape=jax.ShapeDtypeStruct(fields.shape, jnp.float32),
        in_specs=[smem, smem, smem, vmem, vmem],
        out_specs=vmem,
    )(log_rate, activation, heat_release, fields, cell_counts)


def shift_pairs(size, step):
    return [(i, (i + step) % size) for i in range(size)]


def exchange(to_lo, to_hi, axis, size):
    if size % 2:
        from_lo = lax.ppermute(to_hi, axis, shift_pairs(size, 1))
        from_hi = lax.ppermute(to_lo, axis, shift_pairs(size, -1))
        return from_lo, from_hi
    even = lax.axis_index(axis) % 2 == 0
    inner = [(i, i + 1 if i % 2 == 0 else i - 1) for i in range(size)]
    outer = [(i, (i - 1) % size if i % 2 == 0 else (i + 1) % size) for i in range(size)]
    first = lax.ppermute(jnp.where(even, to_hi, to_lo), axis, inner)
    second = lax.ppermute(jnp.where(even, to_lo, to_hi), axis, outer)
    return jnp.where(even, second, first), jnp.where(even, first, second)


def local(state, source_in, counts, diffusivity, log_rate, activation, heat_release):
    nx = lax.axis_size("gx")
    ny = lax.axis_size("gy")
    rows, cx, cy, cz = state.shape
    cell_counts = jnp.broadcast_to(counts[:, :, None], (cx, cy, cz))

    to_xm = jnp.concatenate([state[:, :2], source_in[:, :1]], 1)
    to_xp = jnp.concatenate([state[:, cx - 2:], source_in[:, cx - 1:]], 1)
    from_xm, from_xp = exchange(to_xm, to_xp, "gx", nx)

    early = chemistry(state, cell_counts, log_rate, activation, heat_release)

    def zeros(a, b):
        return jnp.zeros((rows, a, b, cz), jnp.float32)

    wide = jnp.concatenate([from_xm[:, :2], state, from_xp[:, :2]], 1)
    wide_src = jnp.concatenate([from_xm[:, 2:], source_in, from_xp[:, 2:]], 1)
    to_ym = jnp.concatenate([wide[:, 1:-1, :2], wide_src[:, :, :1]], 2)
    to_yp = jnp.concatenate([wide[:, 1:-1, cy - 2:], wide_src[:, :, cy - 1:]], 2)
    from_ym, from_yp = exchange(to_ym, to_yp, "gy", ny)
    next_state, late_source = finish(
        wide, wide_src, from_ym, from_yp, early, cell_counts,
        diffusivity, log_rate, activation, heat_release,
    )
    return (next_state, late_source)


def solution(mesh):
    in_specs = (
        P(None, "gx", "gy", None),
        P(None, "gx", "gy", None),
        P("gx", "gy"),
        P(),
        P(),
        P(),
        P(),
    )
    out_specs = (P(None, "gx", "gy", None), P(None, "gx", "gy", None))
    return jax.shard_map(local, mesh=mesh, in_specs=in_specs, out_specs=out_specs, check_vma=False)
```

```python
import jax
import jax.numpy as jnp
import numpy as np
from jax import lax
from jax.experimental import pallas as pl
from jax.experimental.pallas import tpu as pltpu
from jax.sharding import PartitionSpec as P

time_step = 0.15
reaction_table = (
    (3, 1, (4, 5)),
    (4, 0, (3, 5)),
    (5, 0, (3, 2)),
    (5, 5, (4, 2)),
    (3, 3, (0,)),
    (3, 5, (2,)),
    (4, 4, (1,)),
    (3, 4, (5,)),
    (3, 1, (6,)),
    (6, 3, (0, 1)),
    (6, 3, (5, 5)),
    (6, 4, (1, 5)),
    (6, 5, (2, 1)),
    (6, 6, (7, 1)),
    (7, 9, (5, 5)),
    (7, 3, (2, 5)),
    (7, 3, (6, 0)),
    (7, 4, (5, 6)),
    (7, 5, (6, 2)),
    (0, 9, (3, 3)),
    (2, 9, (3, 5)),
)
SPECIES = 9
CMAX = 8


def stoichiometry():
    change = np.zeros((SPECIES, len(reaction_table)), np.int64)
    for reaction, entry in enumerate(reaction_table):
        change[entry[0], reaction] -= 1
        if entry[1] < SPECIES:
            change[entry[1], reaction] -= 1
        for product in entry[2]:
            change[product, reaction] += 1
    return change


def react(start, cnt, rate_ref, act_ref, heat_ref):
    change = stoichiometry()
    reactions = len(reaction_table)
    temper = start[SPECIES]
    coeffs = [jnp.exp(rate_ref[r] - act_ref[r] / temper) for r in range(reactions)]
    heat = [heat_ref[r] for r in range(reactions)]
    stride = time_step / cnt.astype(jnp.float32)
    cur = list(start)
    for turn in range(CMAX):
        step = jnp.where(turn < cnt, stride, 0.0)
        rates = []
        for r, entry in enumerate(reaction_table):
            term = coeffs[r] * cur[entry[0]]
            if entry[1] < SPECIES:
                term = term * cur[entry[1]]
            rates.append(term)
        new = []
        for s in range(SPECIES):
            total = None
            for r in range(reactions):
                c = int(change[s, r])
                if c == 0:
                    continue
                piece = rates[r] if abs(c) == 1 else rates[r] * float(abs(c))
                if total is None:
                    total = piece if c > 0 else -piece
                elif c > 0:
                    total = total + piece
                else:
                    total = total - piece
            if total is None:
                new.append(cur[s])
            else:
                new.append(cur[s] + step * total)
        heat_total = heat[0] * rates[0]
        for r in range(1, reactions):
            heat_total = heat_total + heat[r] * rates[r]
        new.append(cur[SPECIES] + step * heat_total)
        cur = new
    return [(cur[s] - start[s]) / time_step for s in range(len(start))]


def counts_tile(cnt_ref, x, shape):
    sub = lax.broadcasted_iota(jnp.int32, shape, 0)
    tile = jnp.zeros(shape, jnp.int32)
    for y in range(shape[0]):
        tile = jnp.where(sub == y, cnt_ref[x, y], tile)
    return tile


def chem_kernel(rate_ref, act_ref, heat_ref, u_ref, cnt_ref, o_ref):
    rows = u_ref.shape[0]

    def per_x(x, carry):
        start = [u_ref[s, x] for s in range(rows)]
        cnt = counts_tile(cnt_ref, x, start[0].shape)
        out = react(start, cnt, rate_ref, act_ref, heat_ref)
        for s in range(rows):
            o_ref[s, x] = out[s]
        return carry

    lax.fori_loop(0, u_ref.shape[1], per_x, 0)


def finish_kernel(
    diff_ref, rate_ref, act_ref, heat_ref, par_ref, wide_ref, wsrc_ref, one_ref, two_ref,
    early_ref, cnt_ref, next_ref, late_ref, ext_ref, src_ref, first_ref,
):
    rows, cx, cy, _ = early_ref.shape
    lanes = ext_ref.shape[3]
    even = par_ref[0] == 0
    ext_ref[...] = jnp.zeros(ext_ref.shape, jnp.float32)
    src_ref[...] = jnp.zeros(src_ref.shape, jnp.float32)
    for r in range(rows):
        for e in range(cx + 4):
            ext_ref[r, e, pl.ds(2, cy)] = wide_ref[r, e]
        for i in range(cx + 2):
            one = one_ref[r, i]
            two = two_ref[r, i]
            ym = jnp.where(even, two, one)
            yp = jnp.where(even, one, two)
            ext_ref[r, i + 1, pl.ds(0, 2)] = ym[0:2]
            ext_ref[r, i + 1, pl.ds(cy + 2, 2)] = yp[0:2]
            src_ref[r, i, pl.ds(1, cy)] = wsrc_ref[r, i]
            src_ref[r, i, pl.ds(0, 1)] = ym[2:3]
            src_ref[r, i, pl.ds(cy + 1, 1)] = yp[2:3]

    def laplace(centre, xm, xp, ym, yp):
        beside = xm + xp
        beside = beside + ym + yp
        beside = beside + pltpu.roll(centre, 1, 1) + pltpu.roll(centre, lanes - 1, 1)
        return beside - 6.0 * centre

    def first_row(i, carry):
        e = i + 1
        for r in range(rows):
            for lo in (0, 2):
                centre = ext_ref[r, e, pl.ds(lo + 1, cy)]
                lap = laplace(
                    centre,
                    ext_ref[r, e - 1, pl.ds(lo + 1, cy)],
                    ext_ref[r, e + 1, pl.ds(lo + 1, cy)],
                    ext_ref[r, e, pl.ds(lo, cy)],
                    ext_ref[r, e, pl.ds(lo + 2, cy)],
                )
                first_ref[r, i, pl.ds(lo, cy)] = centre + time_step * (
                    diff_ref[r] * lap + src_ref[r, i, pl.ds(lo, cy)]
                )
        return carry

    lax.fori_loop(0, cx + 2, first_row, 0)

    def box_row(x, carry):
        start = []
        for r in range(rows):
            centre = first_ref[r, x + 1, pl.ds(1, cy)]
            lap = laplace(
                centre,
                first_ref[r, x, pl.ds(1, cy)],
                first_ref[r, x + 2, pl.ds(1, cy)],
                first_ref[r, x + 1, pl.ds(0, cy)],
                first_ref[r, x + 1, pl.ds(2, cy)],
            )
            state = ext_ref[r, x + 2, pl.ds(2, cy)]
            next_ref[r, x] = 0.5 * state + 0.5 * (
                centre + time_step * (diff_ref[r] * lap + early_ref[r, x])
            )
            start.append(centre)
        out = react(start, counts_tile(cnt_ref, x, centre.shape), rate_ref, act_ref, heat_ref)
        for r in range(rows):
            late_ref[r, x] = out[r]
        return carry

    lax.fori_loop(0, cx, box_row, 0)


def finish(parity, wide, wide_src, one, two, early, counts, diffusivity, log_rate, activation, heat_release):
    rows, cx, cy, cz = early.shape
    smem = pl.BlockSpec(memory_space=pltpu.SMEM)
    vmem = pl.BlockSpec(memory_space=pltpu.VMEM)
    box = jax.ShapeDtypeStruct(early.shape, jnp.float32)
    return pl.pallas_call(
        finish_kernel,
        out_shape=(box, box),
        in_specs=[smem] * 5 + [vmem] * 5 + [smem],
        out_specs=(vmem, vmem),
        scratch_shapes=[
            pltpu.VMEM((rows, cx + 4, 2 * cy, cz), jnp.float32),
            pltpu.VMEM((rows, cx + 2, 2 * cy, cz), jnp.float32),
            pltpu.VMEM((rows, cx + 2, 2 * cy, cz), jnp.float32),
        ],
    )(
        diffusivity, log_rate, activation, heat_release, parity,
        wide, wide_src, one, two, early, counts,
    )


def chemistry(fields, cell_counts, log_rate, activation, heat_release):
    smem = pl.BlockSpec(memory_space=pltpu.SMEM)
    vmem = pl.BlockSpec(memory_space=pltpu.VMEM)
    return pl.pallas_call(
        chem_kernel,
        out_shape=jax.ShapeDtypeStruct(fields.shape, jnp.float32),
        in_specs=[smem, smem, smem, vmem, smem],
        out_specs=vmem,
    )(log_rate, activation, heat_release, fields, cell_counts)


def shift_pairs(size, step):
    return [(i, (i + step) % size) for i in range(size)]


def exchange(to_lo, to_hi, axis, size, raw=False):
    if size % 2:
        from_lo = lax.ppermute(to_hi, axis, shift_pairs(size, 1))
        from_hi = lax.ppermute(to_lo, axis, shift_pairs(size, -1))
        return from_lo, from_hi
    even = lax.axis_index(axis) % 2 == 0
    inner = [(i, i + 1 if i % 2 == 0 else i - 1) for i in range(size)]
    outer = [(i, (i - 1) % size if i % 2 == 0 else (i + 1) % size) for i in range(size)]
    first = lax.ppermute(jnp.where(even, to_hi, to_lo), axis, inner)
    second = lax.ppermute(jnp.where(even, to_lo, to_hi), axis, outer)
    if raw:
        return first, second
    return jnp.where(even, second, first), jnp.where(even, first, second)


def local(state, source_in, counts, diffusivity, log_rate, activation, heat_release):
    nx = lax.axis_size("gx")
    ny = lax.axis_size("gy")
    rows, cx, cy, cz = state.shape

    to_xm = jnp.concatenate([state[:, :2], source_in[:, :1]], 1)
    to_xp = jnp.concatenate([state[:, cx - 2:], source_in[:, cx - 1:]], 1)
    from_xm, from_xp = exchange(to_xm, to_xp, "gx", nx)

    early = chemistry(state, counts, log_rate, activation, heat_release)

    def zeros(a, b):
        return jnp.zeros((rows, a, b, cz), jnp.float32)

    wide = jnp.concatenate([from_xm[:, :2], state, from_xp[:, :2]], 1)
    wide_src = jnp.concatenate([from_xm[:, 2:], source_in, from_xp[:, 2:]], 1)
    to_ym = jnp.concatenate([wide[:, 1:-1, :2], wide_src[:, :, :1]], 2)
    to_yp = jnp.concatenate([wide[:, 1:-1, cy - 2:], wide_src[:, :, cy - 1:]], 2)
    if ny % 2:
        one, two = exchange(to_ym, to_yp, "gy", ny)
        parity = jnp.ones((1,), jnp.int32)
    else:
        one, two = exchange(to_ym, to_yp, "gy", ny, raw=True)
        parity = (lax.axis_index("gy") % 2).astype(jnp.int32).reshape(1)
    next_state, late_source = finish(
        parity, wide, wide_src, one, two, early, counts,
        diffusivity, log_rate, activation, heat_release,
    )
    return (next_state, late_source)


def solution(mesh):
    in_specs = (
        P(None, "gx", "gy", None),
        P(None, "gx", "gy", None),
        P("gx", "gy"),
        P(),
        P(),
        P(),
        P(),
    )
    out_specs = (P(None, "gx", "gy", None), P(None, "gx", "gy", None))
    return jax.shard_map(local, mesh=mesh, in_specs=in_specs, out_specs=out_specs, check_vma=False)
```

```python
import jax
import jax.numpy as jnp
import numpy as np
from jax import lax
from jax.experimental import pallas as pl
from jax.experimental.pallas import tpu as pltpu
from jax.sharding import PartitionSpec as P

time_step = 0.15
reaction_table = (
    (3, 1, (4, 5)),
    (4, 0, (3, 5)),
    (5, 0, (3, 2)),
    (5, 5, (4, 2)),
    (3, 3, (0,)),
    (3, 5, (2,)),
    (4, 4, (1,)),
    (3, 4, (5,)),
    (3, 1, (6,)),
    (6, 3, (0, 1)),
    (6, 3, (5, 5)),
    (6, 4, (1, 5)),
    (6, 5, (2, 1)),
    (6, 6, (7, 1)),
    (7, 9, (5, 5)),
    (7, 3, (2, 5)),
    (7, 3, (6, 0)),
    (7, 4, (5, 6)),
    (7, 5, (6, 2)),
    (0, 9, (3, 3)),
    (2, 9, (3, 5)),
)
SPECIES = 9
CMAX = 8


def stoichiometry():
    change = np.zeros((SPECIES, len(reaction_table)), np.int64)
    for reaction, entry in enumerate(reaction_table):
        change[entry[0], reaction] -= 1
        if entry[1] < SPECIES:
            change[entry[1], reaction] -= 1
        for product in entry[2]:
            change[product, reaction] += 1
    return change


def react(start, cnt, rate_ref, act_ref, heat_ref):
    change = stoichiometry()
    reactions = len(reaction_table)
    temper = start[SPECIES]
    coeffs = [jnp.exp(rate_ref[r] - act_ref[r] / temper) for r in range(reactions)]
    heat = [heat_ref[r] for r in range(reactions)]
    stride = time_step / cnt.astype(jnp.float32)
    cur = list(start)
    for turn in range(CMAX):
        active = turn < cnt
        rates = []
        for r, entry in enumerate(reaction_table):
            term = coeffs[r] * cur[entry[0]]
            if entry[1] < SPECIES:
                term = term * cur[entry[1]]
            rates.append(term)
        new = []
        for s in range(SPECIES):
            total = None
            for r in range(reactions):
                c = int(change[s, r])
                if c == 0:
                    continue
                piece = rates[r] if abs(c) == 1 else rates[r] * float(abs(c))
                if total is None:
                    total = piece if c > 0 else -piece
                elif c > 0:
                    total = total + piece
                else:
                    total = total - piece
            if total is None:
                new.append(cur[s])
            else:
                new.append(jnp.where(active, cur[s] + stride * total, cur[s]))
        heat_total = heat[0] * rates[0]
        for r in range(1, reactions):
            heat_total = heat_total + heat[r] * rates[r]
        new.append(jnp.where(active, cur[SPECIES] + stride * heat_total, cur[SPECIES]))
        cur = new
    return [(cur[s] - start[s]) / time_step for s in range(len(start))]


def counts_tile(cnt_ref, x, shape):
    sub = lax.broadcasted_iota(jnp.int32, shape, 0)
    tile = jnp.zeros(shape, jnp.int32)
    for y in range(shape[0]):
        tile = jnp.where(sub == y, cnt_ref[x, y], tile)
    return tile


def chem_kernel(rate_ref, act_ref, heat_ref, hbm_ref, cnt_ref, o_ref, u_ref, sem):
    rows = u_ref.shape[0]
    copy = pltpu.make_async_copy(hbm_ref, u_ref, sem)
    copy.start()
    copy.wait()

    def per_x(x, carry):
        start = [u_ref[s, x] for s in range(rows)]
        cnt = counts_tile(cnt_ref, x, start[0].shape)
        out = react(start, cnt, rate_ref, act_ref, heat_ref)
        for s in range(rows):
            o_ref[s, x] = out[s]
        return carry

    lax.fori_loop(0, u_ref.shape[1], per_x, 0)


def finish_kernel(
    diff_ref, rate_ref, act_ref, heat_ref, ext_ref, src_ref, early_ref, cnt_ref,
    next_ref, late_ref, first_ref,
):
    rows, cx, cy, _ = early_ref.shape
    lanes = ext_ref.shape[3]

    def laplace(centre, xm, xp, ym, yp):
        beside = xm + xp
        beside = beside + ym + yp
        beside = beside + pltpu.roll(centre, 1, 1) + pltpu.roll(centre, lanes - 1, 1)
        return beside - 6.0 * centre

    def first_row(i, carry):
        e = i + 1
        for r in range(rows):
            for lo in (0, 2):
                centre = ext_ref[r, e, pl.ds(lo + 1, cy)]
                lap = laplace(
                    centre,
                    ext_ref[r, e - 1, pl.ds(lo + 1, cy)],
                    ext_ref[r, e + 1, pl.ds(lo + 1, cy)],
                    ext_ref[r, e, pl.ds(lo, cy)],
                    ext_ref[r, e, pl.ds(lo + 2, cy)],
                )
                first_ref[r, i, pl.ds(lo, cy)] = centre + time_step * (
                    diff_ref[r] * lap + src_ref[r, i, pl.ds(lo, cy)]
                )
        return carry

    lax.fori_loop(0, cx + 2, first_row, 0)

    def box_row(x, carry):
        start = []
        for r in range(rows):
            centre = first_ref[r, x + 1, pl.ds(1, cy)]
            lap = laplace(
                centre,
                first_ref[r, x, pl.ds(1, cy)],
                first_ref[r, x + 2, pl.ds(1, cy)],
                first_ref[r, x + 1, pl.ds(0, cy)],
                first_ref[r, x + 1, pl.ds(2, cy)],
            )
            state = ext_ref[r, x + 2, pl.ds(2, cy)]
            next_ref[r, x] = 0.5 * state + 0.5 * (
                centre + time_step * (diff_ref[r] * lap + early_ref[r, x])
            )
            start.append(centre)
        out = react(start, counts_tile(cnt_ref, x, centre.shape), rate_ref, act_ref, heat_ref)
        for r in range(rows):
            late_ref[r, x] = out[r]
        return carry

    lax.fori_loop(0, cx, box_row, 0)


def finish(ext, src, early, cell_counts, diffusivity, log_rate, activation, heat_release):
    rows, cx, cy, cz = early.shape
    smem = pl.BlockSpec(memory_space=pltpu.SMEM)
    vmem = pl.BlockSpec(memory_space=pltpu.VMEM)
    box = jax.ShapeDtypeStruct(early.shape, jnp.float32)
    return pl.pallas_call(
        finish_kernel,
        out_shape=(box, box),
        in_specs=[smem, smem, smem, smem, vmem, vmem, vmem, smem],
        out_specs=(vmem, vmem),
        scratch_shapes=[pltpu.VMEM((rows, cx + 2, 2 * cy, cz), jnp.float32)],
    )(diffusivity, log_rate, activation, heat_release, ext, src, early, cell_counts)


def chemistry(fields, cell_counts, log_rate, activation, heat_release):
    smem = pl.BlockSpec(memory_space=pltpu.SMEM)
    vmem = pl.BlockSpec(memory_space=pltpu.VMEM)
    return pl.pallas_call(
        chem_kernel,
        out_shape=jax.ShapeDtypeStruct(fields.shape, jnp.float32),
        in_specs=[smem, smem, smem, pl.BlockSpec(memory_space=pl.ANY), smem],
        out_specs=vmem,
        scratch_shapes=[
            pltpu.VMEM(fields.shape, jnp.float32),
            pltpu.SemaphoreType.DMA(()),
        ],
    )(log_rate, activation, heat_release, fields, cell_counts)


def shift_pairs(size, step):
    return [(i, (i + step) % size) for i in range(size)]


def exchange(to_lo, to_hi, axis, size):
    if size % 2:
        from_lo = lax.ppermute(to_hi, axis, shift_pairs(size, 1))
        from_hi = lax.ppermute(to_lo, axis, shift_pairs(size, -1))
        return from_lo, from_hi
    even = lax.axis_index(axis) % 2 == 0
    inner = [(i, i + 1 if i % 2 == 0 else i - 1) for i in range(size)]
    outer = [(i, (i - 1) % size if i % 2 == 0 else (i + 1) % size) for i in range(size)]
    first = lax.ppermute(jnp.where(even, to_hi, to_lo), axis, inner)
    second = lax.ppermute(jnp.where(even, to_lo, to_hi), axis, outer)
    return jnp.where(even, second, first), jnp.where(even, first, second)


def local(state, source_in, counts, diffusivity, log_rate, activation, heat_release):
    nx = lax.axis_size("gx")
    ny = lax.axis_size("gy")
    rows, cx, cy, cz = state.shape
    cell_counts = counts

    to_xm = jnp.concatenate([state[:, :2], source_in[:, :1]], 1)
    to_xp = jnp.concatenate([state[:, cx - 2:], source_in[:, cx - 1:]], 1)
    from_xm, from_xp = exchange(to_xm, to_xp, "gx", nx)

    early = chemistry(state, cell_counts, log_rate, activation, heat_release)

    def zeros(a, b):
        return jnp.zeros((rows, a, b, cz), jnp.float32)

    wide = jnp.concatenate([from_xm[:, :2], state, from_xp[:, :2]], 1)
    wide_src = jnp.concatenate([from_xm[:, 2:], source_in, from_xp[:, 2:]], 1)
    to_ym = jnp.concatenate([wide[:, 1:-1, :2], wide_src[:, :, :1]], 2)
    to_yp = jnp.concatenate([wide[:, 1:-1, cy - 2:], wide_src[:, :, cy - 1:]], 2)
    from_ym, from_yp = exchange(to_ym, to_yp, "gy", ny)
    ext = jnp.concatenate(
        [
            jnp.concatenate([zeros(1, 2), wide[:, :1], zeros(1, 2)], 2),
            jnp.concatenate([from_ym[:, :, :2], wide[:, 1:-1], from_yp[:, :, :2]], 2),
            jnp.concatenate([zeros(1, 2), wide[:, -1:], zeros(1, 2)], 2),
        ],
        1,
    )
    src = jnp.concatenate([from_ym[:, :, 2:], wide_src, from_yp[:, :, 2:]], 2)
    next_state, late_source = finish(
        ext, src, early, cell_counts, diffusivity, log_rate, activation, heat_release
    )
    return (next_state, late_source)


def solution(mesh):
    in_specs = (
        P(None, "gx", "gy", None),
        P(None, "gx", "gy", None),
        P("gx", "gy"),
        P(),
        P(),
        P(),
        P(),
    )
    out_specs = (P(None, "gx", "gy", None), P(None, "gx", "gy", None))
    return jax.shard_map(local, mesh=mesh, in_specs=in_specs, out_specs=out_specs, check_vma=False)
```

```python
import jax
import jax.numpy as jnp
import numpy as np
from jax import lax
from jax.experimental import pallas as pl
from jax.experimental.pallas import tpu as pltpu
from jax.sharding import PartitionSpec as P

time_step = 0.15
reaction_table = (
    (3, 1, (4, 5)),
    (4, 0, (3, 5)),
    (5, 0, (3, 2)),
    (5, 5, (4, 2)),
    (3, 3, (0,)),
    (3, 5, (2,)),
    (4, 4, (1,)),
    (3, 4, (5,)),
    (3, 1, (6,)),
    (6, 3, (0, 1)),
    (6, 3, (5, 5)),
    (6, 4, (1, 5)),
    (6, 5, (2, 1)),
    (6, 6, (7, 1)),
    (7, 9, (5, 5)),
    (7, 3, (2, 5)),
    (7, 3, (6, 0)),
    (7, 4, (5, 6)),
    (7, 5, (6, 2)),
    (0, 9, (3, 3)),
    (2, 9, (3, 5)),
)
SPECIES = 9
CMAX = 8


def stoichiometry():
    change = np.zeros((SPECIES, len(reaction_table)), np.int64)
    for reaction, entry in enumerate(reaction_table):
        change[entry[0], reaction] -= 1
        if entry[1] < SPECIES:
            change[entry[1], reaction] -= 1
        for product in entry[2]:
            change[product, reaction] += 1
    return change


def react(start, cnt, rate_ref, act_ref, heat_ref):
    change = stoichiometry()
    reactions = len(reaction_table)
    temper = start[SPECIES]
    coeffs = [jnp.exp(rate_ref[r] - act_ref[r] / temper) for r in range(reactions)]
    heat = [heat_ref[r] for r in range(reactions)]
    stride = time_step / cnt.astype(jnp.float32)
    cur = list(start)
    for turn in range(CMAX):
        active = turn < cnt
        rates = []
        for r, entry in enumerate(reaction_table):
            term = coeffs[r] * cur[entry[0]]
            if entry[1] < SPECIES:
                term = term * cur[entry[1]]
            rates.append(term)
        new = []
        for s in range(SPECIES):
            total = None
            for r in range(reactions):
                c = int(change[s, r])
                if c == 0:
                    continue
                piece = rates[r] if abs(c) == 1 else rates[r] * float(abs(c))
                if total is None:
                    total = piece if c > 0 else -piece
                elif c > 0:
                    total = total + piece
                else:
                    total = total - piece
            if total is None:
                new.append(cur[s])
            else:
                new.append(jnp.where(active, cur[s] + stride * total, cur[s]))
        heat_total = heat[0] * rates[0]
        for r in range(1, reactions):
            heat_total = heat_total + heat[r] * rates[r]
        new.append(jnp.where(active, cur[SPECIES] + stride * heat_total, cur[SPECIES]))
        cur = new
    return [(cur[s] - start[s]) / time_step for s in range(len(start))]


def chem_kernel(rate_ref, act_ref, heat_ref, u_ref, cnt_ref, o_ref):
    rows = u_ref.shape[0]

    def per_x(x, carry):
        start = [u_ref[s, x] for s in range(rows)]
        out = react(start, cnt_ref[x], rate_ref, act_ref, heat_ref)
        for s in range(rows):
            o_ref[s, x] = out[s]
        return carry

    lax.fori_loop(0, u_ref.shape[1], per_x, 0)


def finish_kernel(
    diff_ref, rate_ref, act_ref, heat_ref, ext_ref, src_ref, early_ref, cnt_ref,
    next_ref, late_ref, first_ref,
):
    rows, cx, cy, _ = early_ref.shape
    lanes = ext_ref.shape[3]

    def laplace(centre, xm, xp, ym, yp):
        beside = xm + xp
        beside = beside + ym + yp
        beside = beside + pltpu.roll(centre, 1, 1) + pltpu.roll(centre, lanes - 1, 1)
        return beside - 6.0 * centre

    def first_row(i, carry):
        e = i + 1
        for r in range(rows):
            for lo in (0, 2):
                centre = ext_ref[r, e, pl.ds(lo + 1, cy)]
                lap = laplace(
                    centre,
                    ext_ref[r, e - 1, pl.ds(lo + 1, cy)],
                    ext_ref[r, e + 1, pl.ds(lo + 1, cy)],
                    ext_ref[r, e, pl.ds(lo, cy)],
                    ext_ref[r, e, pl.ds(lo + 2, cy)],
                )
                first_ref[r, i, pl.ds(lo, cy)] = centre + time_step * (
                    diff_ref[r] * lap + src_ref[r, i, pl.ds(lo, cy)]
                )
        return carry

    lax.fori_loop(0, cx + 2, first_row, 0)

    def box_row(x, carry):
        start = []
        for r in range(rows):
            centre = first_ref[r, x + 1, pl.ds(1, cy)]
            lap = laplace(
                centre,
                first_ref[r, x, pl.ds(1, cy)],
                first_ref[r, x + 2, pl.ds(1, cy)],
                first_ref[r, x + 1, pl.ds(0, cy)],
                first_ref[r, x + 1, pl.ds(2, cy)],
            )
            state = ext_ref[r, x + 2, pl.ds(2, cy)]
            next_ref[r, x] = 0.5 * state + 0.5 * (
                centre + time_step * (diff_ref[r] * lap + early_ref[r, x])
            )
            start.append(centre)
        out = react(start, cnt_ref[x], rate_ref, act_ref, heat_ref)
        for r in range(rows):
            late_ref[r, x] = out[r]
        return carry

    lax.fori_loop(0, cx, box_row, 0)


def finish(ext, src, early, cell_counts, diffusivity, log_rate, activation, heat_release):
    rows, cx, cy, cz = early.shape
    smem = pl.BlockSpec(memory_space=pltpu.SMEM)
    vmem = pl.BlockSpec(memory_space=pltpu.VMEM)
    box = jax.ShapeDtypeStruct(early.shape, jnp.float32)
    return pl.pallas_call(
        finish_kernel,
        out_shape=(box, box),
        in_specs=[smem, smem, smem, smem, vmem, vmem, vmem, vmem],
        out_specs=(vmem, vmem),
        scratch_shapes=[pltpu.VMEM((rows, cx + 2, 2 * cy, cz), jnp.float32)],
    )(diffusivity, log_rate, activation, heat_release, ext, src, early, cell_counts)


def chemistry(fields, cell_counts, log_rate, activation, heat_release):
    smem = pl.BlockSpec(memory_space=pltpu.SMEM)
    vmem = pl.BlockSpec(memory_space=pltpu.VMEM)
    return pl.pallas_call(
        chem_kernel,
        out_shape=jax.ShapeDtypeStruct(fields.shape, jnp.float32),
        in_specs=[smem, smem, smem, vmem, vmem],
        out_specs=vmem,
    )(log_rate, activation, heat_release, fields, cell_counts)


def shift_pairs(size, step):
    return [(i, (i + step) % size) for i in range(size)]


def exchange(to_lo, to_hi, axis, size):
    if size % 2:
        from_lo = lax.ppermute(to_hi, axis, shift_pairs(size, 1))
        from_hi = lax.ppermute(to_lo, axis, shift_pairs(size, -1))
        return from_lo, from_hi
    even = lax.axis_index(axis) % 2 == 0
    inner = [(i, i + 1 if i % 2 == 0 else i - 1) for i in range(size)]
    outer = [(i, (i - 1) % size if i % 2 == 0 else (i + 1) % size) for i in range(size)]
    first = lax.ppermute(jnp.where(even, to_hi, to_lo), axis, inner)
    second = lax.ppermute(jnp.where(even, to_lo, to_hi), axis, outer)
    return jnp.where(even, second, first), jnp.where(even, first, second)


def exchange_edges(state, source_in, axis, size):
    cx = state.shape[1]
    if size % 2:
        to_lo = jnp.concatenate([state[:, :2], source_in[:, :1]], 1)
        to_hi = jnp.concatenate([state[:, cx - 2:], source_in[:, cx - 1:]], 1)
        return exchange(to_lo, to_hi, axis, size)
    even = lax.axis_index(axis) % 2 == 0

    def rows_from(high):
        top = jnp.where(high, cx - 2, 0)
        return jnp.concatenate(
            [
                lax.dynamic_slice_in_dim(state, top, 2, 1),
                lax.dynamic_slice_in_dim(source_in, jnp.where(high, cx - 1, 0), 1, 1),
            ],
            1,
        )

    inner = [(i, i + 1 if i % 2 == 0 else i - 1) for i in range(size)]
    outer = [(i, (i - 1) % size if i % 2 == 0 else (i + 1) % size) for i in range(size)]
    first = lax.ppermute(rows_from(even), axis, inner)
    second = lax.ppermute(rows_from(jnp.logical_not(even)), axis, outer)
    return jnp.where(even, second, first), jnp.where(even, first, second)


def local(state, source_in, counts, diffusivity, log_rate, activation, heat_release):
    nx = lax.axis_size("gx")
    ny = lax.axis_size("gy")
    rows, cx, cy, cz = state.shape
    cell_counts = jnp.broadcast_to(counts[:, :, None], (cx, cy, cz))

    from_xm, from_xp = exchange_edges(state, source_in, "gx", nx)

    early = chemistry(state, cell_counts, log_rate, activation, heat_release)

    def zeros(a, b):
        return jnp.zeros((rows, a, b, cz), jnp.float32)

    wide = jnp.concatenate([from_xm[:, :2], state, from_xp[:, :2]], 1)
    wide_src = jnp.concatenate([from_xm[:, 2:], source_in, from_xp[:, 2:]], 1)
    to_ym = jnp.concatenate([wide[:, 1:-1, :2], wide_src[:, :, :1]], 2)
    to_yp = jnp.concatenate([wide[:, 1:-1, cy - 2:], wide_src[:, :, cy - 1:]], 2)
    from_ym, from_yp = exchange(to_ym, to_yp, "gy", ny)
    ext = jnp.concatenate(
        [
            jnp.concatenate([zeros(1, 2), wide[:, :1], zeros(1, 2)], 2),
            jnp.concatenate([from_ym[:, :, :2], wide[:, 1:-1], from_yp[:, :, :2]], 2),
            jnp.concatenate([zeros(1, 2), wide[:, -1:], zeros(1, 2)], 2),
        ],
        1,
    )
    src = jnp.concatenate([from_ym[:, :, 2:], wide_src, from_yp[:, :, 2:]], 2)
    next_state, late_source = finish(
        ext, src, early, cell_counts, diffusivity, log_rate, activation, heat_release
    )
    return (next_state, late_source)


def solution(mesh):
    in_specs = (
        P(None, "gx", "gy", None),
        P(None, "gx", "gy", None),
        P("gx", "gy"),
        P(),
        P(),
        P(),
        P(),
    )
    out_specs = (P(None, "gx", "gy", None), P(None, "gx", "gy", None))
    return jax.shard_map(local, mesh=mesh, in_specs=in_specs, out_specs=out_specs, check_vma=False)
```

```python
import jax
import jax.numpy as jnp
import numpy as np
from jax import lax
from jax.experimental import pallas as pl
from jax.experimental.pallas import tpu as pltpu
from jax.sharding import PartitionSpec as P

time_step = 0.15
reaction_table = (
    (3, 1, (4, 5)),
    (4, 0, (3, 5)),
    (5, 0, (3, 2)),
    (5, 5, (4, 2)),
    (3, 3, (0,)),
    (3, 5, (2,)),
    (4, 4, (1,)),
    (3, 4, (5,)),
    (3, 1, (6,)),
    (6, 3, (0, 1)),
    (6, 3, (5, 5)),
    (6, 4, (1, 5)),
    (6, 5, (2, 1)),
    (6, 6, (7, 1)),
    (7, 9, (5, 5)),
    (7, 3, (2, 5)),
    (7, 3, (6, 0)),
    (7, 4, (5, 6)),
    (7, 5, (6, 2)),
    (0, 9, (3, 3)),
    (2, 9, (3, 5)),
)
SPECIES = 9
CMAX = 8


def stoichiometry():
    change = np.zeros((SPECIES, len(reaction_table)), np.int64)
    for reaction, entry in enumerate(reaction_table):
        change[entry[0], reaction] -= 1
        if entry[1] < SPECIES:
            change[entry[1], reaction] -= 1
        for product in entry[2]:
            change[product, reaction] += 1
    return change


def react(start, cnt, rate_ref, act_ref, heat_ref):
    change = stoichiometry()
    reactions = len(reaction_table)
    temper = start[SPECIES]
    coeffs = [jnp.exp(rate_ref[r] - act_ref[r] / temper) for r in range(reactions)]
    heat = [heat_ref[r] for r in range(reactions)]
    stride = time_step / cnt.astype(jnp.float32)
    cur = list(start)
    for turn in range(CMAX):
        active = turn < cnt
        rates = []
        for r, entry in enumerate(reaction_table):
            term = coeffs[r] * cur[entry[0]]
            if entry[1] < SPECIES:
                term = term * cur[entry[1]]
            rates.append(term)
        new = []
        for s in range(SPECIES):
            total = None
            for r in range(reactions):
                c = int(change[s, r])
                if c == 0:
                    continue
                piece = rates[r] if abs(c) == 1 else rates[r] * float(abs(c))
                if total is None:
                    total = piece if c > 0 else -piece
                elif c > 0:
                    total = total + piece
                else:
                    total = total - piece
            if total is None:
                new.append(cur[s])
            else:
                new.append(jnp.where(active, cur[s] + stride * total, cur[s]))
        heat_total = heat[0] * rates[0]
        for r in range(1, reactions):
            heat_total = heat_total + heat[r] * rates[r]
        new.append(jnp.where(active, cur[SPECIES] + stride * heat_total, cur[SPECIES]))
        cur = new
    return [(cur[s] - start[s]) / time_step for s in range(len(start))]


def counts_tile(cnt_ref, x, shape):
    sub = lax.broadcasted_iota(jnp.int32, shape, 0)
    tile = jnp.zeros(shape, jnp.int32)
    for y in range(shape[0]):
        tile = jnp.where(sub == y, cnt_ref[x, y], tile)
    return tile


def chem_kernel(rate_ref, act_ref, heat_ref, u_ref, cnt_ref, o_ref):
    rows = u_ref.shape[0]

    def per_x(x, carry):
        start = [u_ref[s, x] for s in range(rows)]
        cnt = counts_tile(cnt_ref, x, start[0].shape)
        out = react(start, cnt, rate_ref, act_ref, heat_ref)
        for s in range(rows):
            o_ref[s, x] = out[s]
        return carry

    lax.fori_loop(0, u_ref.shape[1], per_x, 0)


def finish_kernel(
    diff_ref, rate_ref, act_ref, heat_ref, ext_ref, src_ref, early_ref, cnt_ref,
    next_ref, late_ref, first_ref,
):
    rows, cx, cy, _ = early_ref.shape
    lanes = ext_ref.shape[3]

    def laplace(centre, xm, xp, ym, yp):
        beside = xm + xp
        beside = beside + ym + yp
        beside = beside + pltpu.roll(centre, 1, 1) + pltpu.roll(centre, lanes - 1, 1)
        return beside - 6.0 * centre

    def first_row(i, carry):
        e = i + 1
        for r in range(rows):
            for lo in (0, 2):
                centre = ext_ref[r, e, pl.ds(lo + 1, cy)]
                lap = laplace(
                    centre,
                    ext_ref[r, e - 1, pl.ds(lo + 1, cy)],
                    ext_ref[r, e + 1, pl.ds(lo + 1, cy)],
                    ext_ref[r, e, pl.ds(lo, cy)],
                    ext_ref[r, e, pl.ds(lo + 2, cy)],
                )
                first_ref[r, i, pl.ds(lo, cy)] = centre + time_step * (
                    diff_ref[r] * lap + src_ref[r, i, pl.ds(lo, cy)]
                )
        return carry

    lax.fori_loop(0, cx + 2, first_row, 0)

    def box_row(x, carry):
        start = []
        for r in range(rows):
            centre = first_ref[r, x + 1, pl.ds(1, cy)]
            lap = laplace(
                centre,
                first_ref[r, x, pl.ds(1, cy)],
                first_ref[r, x + 2, pl.ds(1, cy)],
                first_ref[r, x + 1, pl.ds(0, cy)],
                first_ref[r, x + 1, pl.ds(2, cy)],
            )
            state = ext_ref[r, x + 2, pl.ds(2, cy)]
            next_ref[r, x] = 0.5 * state + 0.5 * (
                centre + time_step * (diff_ref[r] * lap + early_ref[r, x])
            )
            start.append(centre)
        out = react(start, counts_tile(cnt_ref, x, centre.shape), rate_ref, act_ref, heat_ref)
        for r in range(rows):
            late_ref[r, x] = out[r]
        return carry

    lax.fori_loop(0, cx, box_row, 0)


def finish(ext, src, early, cell_counts, diffusivity, log_rate, activation, heat_release):
    rows, cx, cy, cz = early.shape
    smem = pl.BlockSpec(memory_space=pltpu.SMEM)
    vmem = pl.BlockSpec(memory_space=pltpu.VMEM)
    box = jax.ShapeDtypeStruct(early.shape, jnp.float32)
    return pl.pallas_call(
        finish_kernel,
        out_shape=(box, box),
        in_specs=[smem, smem, smem, smem, vmem, vmem, vmem, smem],
        out_specs=(vmem, vmem),
        scratch_shapes=[pltpu.VMEM((rows, cx + 2, 2 * cy, cz), jnp.float32)],
    )(diffusivity, log_rate, activation, heat_release, ext, src, early, cell_counts)


def chemistry(fields, cell_counts, log_rate, activation, heat_release):
    smem = pl.BlockSpec(memory_space=pltpu.SMEM)
    vmem = pl.BlockSpec(memory_space=pltpu.VMEM)
    return pl.pallas_call(
        chem_kernel,
        out_shape=jax.ShapeDtypeStruct(fields.shape, jnp.float32),
        in_specs=[smem, smem, smem, vmem, smem],
        out_specs=vmem,
    )(log_rate, activation, heat_release, fields, cell_counts)


def shift_pairs(size, step):
    return [(i, (i + step) % size) for i in range(size)]


def exchange(to_lo, to_hi, axis, size):
    if size % 2:
        from_lo = lax.ppermute(to_hi, axis, shift_pairs(size, 1))
        from_hi = lax.ppermute(to_lo, axis, shift_pairs(size, -1))
        return from_lo, from_hi
    even = lax.axis_index(axis) % 2 == 0
    inner = [(i, i + 1 if i % 2 == 0 else i - 1) for i in range(size)]
    outer = [(i, (i - 1) % size if i % 2 == 0 else (i + 1) % size) for i in range(size)]
    first = lax.ppermute(jnp.where(even, to_hi, to_lo), axis, inner)
    second = lax.ppermute(jnp.where(even, to_lo, to_hi), axis, outer)
    return jnp.where(even, second, first), jnp.where(even, first, second)


def local(state, source_in, counts, diffusivity, log_rate, activation, heat_release):
    nx = lax.axis_size("gx")
    ny = lax.axis_size("gy")
    rows, cx, cy, cz = state.shape
    cell_counts = counts

    to_xm = jnp.concatenate([state[:, :2], source_in[:, :1]], 1)
    to_xp = jnp.concatenate([state[:, cx - 2:], source_in[:, cx - 1:]], 1)
    from_xm, from_xp = exchange(to_xm, to_xp, "gx", nx)

    early = chemistry(state, cell_counts, log_rate, activation, heat_release)

    def zeros(a, b):
        return jnp.zeros((rows, a, b, cz), jnp.float32)

    wide = jnp.concatenate([from_xm[:, :2], state, from_xp[:, :2]], 1)
    wide_src = jnp.concatenate([from_xm[:, 2:], source_in, from_xp[:, 2:]], 1)
    to_ym = jnp.concatenate([wide[:, 1:-1, :2], wide_src[:, :, :1]], 2)
    to_yp = jnp.concatenate([wide[:, 1:-1, cy - 2:], wide_src[:, :, cy - 1:]], 2)
    from_ym, from_yp = exchange(to_ym, to_yp, "gy", ny)
    ext = jnp.concatenate(
        [
            jnp.concatenate([zeros(1, 2), wide[:, :1], zeros(1, 2)], 2),
            jnp.concatenate([from_ym[:, :, :2], wide[:, 1:-1], from_yp[:, :, :2]], 2),
            jnp.concatenate([zeros(1, 2), wide[:, -1:], zeros(1, 2)], 2),
        ],
        1,
    )
    src = jnp.concatenate([from_ym[:, :, 2:], wide_src, from_yp[:, :, 2:]], 2)
    next_state, late_source = finish(
        ext, src, early, cell_counts, diffusivity, log_rate, activation, heat_release
    )
    return (next_state, late_source)


def solution(mesh):
    in_specs = (
        P(None, "gx", "gy", None),
        P(None, "gx", "gy", None),
        P("gx", "gy"),
        P(),
        P(),
        P(),
        P(),
    )
    out_specs = (P(None, "gx", "gy", None), P(None, "gx", "gy", None))
    return jax.shard_map(local, mesh=mesh, in_specs=in_specs, out_specs=out_specs, check_vma=False)
```

```python
import jax
import jax.numpy as jnp
import numpy as np
from jax import lax
from jax.experimental import pallas as pl
from jax.experimental.pallas import tpu as pltpu
from jax.sharding import PartitionSpec as P

time_step = 0.15
reaction_table = (
    (3, 1, (4, 5)),
    (4, 0, (3, 5)),
    (5, 0, (3, 2)),
    (5, 5, (4, 2)),
    (3, 3, (0,)),
    (3, 5, (2,)),
    (4, 4, (1,)),
    (3, 4, (5,)),
    (3, 1, (6,)),
    (6, 3, (0, 1)),
    (6, 3, (5, 5)),
    (6, 4, (1, 5)),
    (6, 5, (2, 1)),
    (6, 6, (7, 1)),
    (7, 9, (5, 5)),
    (7, 3, (2, 5)),
    (7, 3, (6, 0)),
    (7, 4, (5, 6)),
    (7, 5, (6, 2)),
    (0, 9, (3, 3)),
    (2, 9, (3, 5)),
)
SPECIES = 9
CMAX = 8


def stoichiometry():
    change = np.zeros((SPECIES, len(reaction_table)), np.int64)
    for reaction, entry in enumerate(reaction_table):
        change[entry[0], reaction] -= 1
        if entry[1] < SPECIES:
            change[entry[1], reaction] -= 1
        for product in entry[2]:
            change[product, reaction] += 1
    return change


def react(start, cnt, rate_ref, act_ref, heat_ref):
    change = stoichiometry()
    reactions = len(reaction_table)
    temper = start[SPECIES]
    coeffs = [jnp.exp(rate_ref[r] - act_ref[r] / temper) for r in range(reactions)]
    heat = [heat_ref[r] for r in range(reactions)]
    stride = time_step / cnt.astype(jnp.float32)
    cur = list(start)
    for turn in range(CMAX):
        step = jnp.where(turn < cnt, stride, 0.0)
        rates = []
        for r, entry in enumerate(reaction_table):
            term = coeffs[r] * cur[entry[0]]
            if entry[1] < SPECIES:
                term = term * cur[entry[1]]
            rates.append(term)
        new = []
        for s in range(SPECIES):
            total = None
            for r in range(reactions):
                c = int(change[s, r])
                if c == 0:
                    continue
                piece = rates[r] if abs(c) == 1 else rates[r] * float(abs(c))
                if total is None:
                    total = piece if c > 0 else -piece
                elif c > 0:
                    total = total + piece
                else:
                    total = total - piece
            if total is None:
                new.append(cur[s])
            else:
                new.append(cur[s] + step * total)
        heat_total = heat[0] * rates[0]
        for r in range(1, reactions):
            heat_total = heat_total + heat[r] * rates[r]
        new.append(cur[SPECIES] + step * heat_total)
        cur = new
    return [(cur[s] - start[s]) / time_step for s in range(len(start))]


def chem_kernel(rate_ref, act_ref, heat_ref, u_ref, cnt_ref, o_ref):
    rows = u_ref.shape[0]

    def per_x(x, carry):
        start = [u_ref[s, x] for s in range(rows)]
        out = react(start, cnt_ref[x], rate_ref, act_ref, heat_ref)
        for s in range(rows):
            o_ref[s, x] = out[s]
        return carry

    lax.fori_loop(0, u_ref.shape[1], per_x, 0)


def finish_kernel(
    diff_ref, rate_ref, act_ref, heat_ref, ext_ref, src_ref, early_ref, cnt_ref,
    next_ref, late_ref, first_ref,
):
    rows, cx, cy, _ = early_ref.shape
    lanes = ext_ref.shape[3]

    def laplace(centre, xm, xp, ym, yp):
        beside = xm + xp
        beside = beside + ym + yp
        beside = beside + pltpu.roll(centre, 1, 1) + pltpu.roll(centre, lanes - 1, 1)
        return beside - 6.0 * centre

    def first_row(i, carry):
        e = i + 1
        for r in range(rows):
            for lo in (0, 2):
                centre = ext_ref[r, e, pl.ds(lo + 1, cy)]
                lap = laplace(
                    centre,
                    ext_ref[r, e - 1, pl.ds(lo + 1, cy)],
                    ext_ref[r, e + 1, pl.ds(lo + 1, cy)],
                    ext_ref[r, e, pl.ds(lo, cy)],
                    ext_ref[r, e, pl.ds(lo + 2, cy)],
                )
                first_ref[r, i, pl.ds(lo, cy)] = centre + time_step * (
                    diff_ref[r] * lap + src_ref[r, i, pl.ds(lo, cy)]
                )
        return carry

    lax.fori_loop(0, cx + 2, first_row, 0)

    def box_row(x, carry):
        start = []
        for r in range(rows):
            centre = first_ref[r, x + 1, pl.ds(1, cy)]
            lap = laplace(
                centre,
                first_ref[r, x, pl.ds(1, cy)],
                first_ref[r, x + 2, pl.ds(1, cy)],
                first_ref[r, x + 1, pl.ds(0, cy)],
                first_ref[r, x + 1, pl.ds(2, cy)],
            )
            state = ext_ref[r, x + 2, pl.ds(2, cy)]
            next_ref[r, x] = 0.5 * state + 0.5 * (
                centre + time_step * (diff_ref[r] * lap + early_ref[r, x])
            )
            start.append(centre)
        out = react(start, cnt_ref[x], rate_ref, act_ref, heat_ref)
        for r in range(rows):
            late_ref[r, x] = out[r]
        return carry

    lax.fori_loop(0, cx, box_row, 0)


def finish(ext, src, early, cell_counts, diffusivity, log_rate, activation, heat_release):
    rows, cx, cy, cz = early.shape
    smem = pl.BlockSpec(memory_space=pltpu.SMEM)
    vmem = pl.BlockSpec(memory_space=pltpu.VMEM)
    box = jax.ShapeDtypeStruct(early.shape, jnp.float32)
    return pl.pallas_call(
        finish_kernel,
        out_shape=(box, box),
        in_specs=[smem, smem, smem, smem, vmem, vmem, vmem, vmem],
        out_specs=(vmem, vmem),
        scratch_shapes=[pltpu.VMEM((rows, cx + 2, 2 * cy, cz), jnp.float32)],
    )(diffusivity, log_rate, activation, heat_release, ext, src, early, cell_counts)


def chemistry(fields, cell_counts, log_rate, activation, heat_release):
    smem = pl.BlockSpec(memory_space=pltpu.SMEM)
    vmem = pl.BlockSpec(memory_space=pltpu.VMEM)
    return pl.pallas_call(
        chem_kernel,
        out_shape=jax.ShapeDtypeStruct(fields.shape, jnp.float32),
        in_specs=[smem, smem, smem, vmem, vmem],
        out_specs=vmem,
    )(log_rate, activation, heat_release, fields, cell_counts)


def shift_pairs(size, step):
    return [(i, (i + step) % size) for i in range(size)]


def exchange(to_lo, to_hi, axis, size):
    if size % 2:
        from_lo = lax.ppermute(to_hi, axis, shift_pairs(size, 1))
        from_hi = lax.ppermute(to_lo, axis, shift_pairs(size, -1))
        return from_lo, from_hi
    even = lax.axis_index(axis) % 2 == 0
    inner = [(i, i + 1 if i % 2 == 0 else i - 1) for i in range(size)]
    outer = [(i, (i - 1) % size if i % 2 == 0 else (i + 1) % size) for i in range(size)]
    first = lax.ppermute(jnp.where(even, to_hi, to_lo), axis, inner)
    second = lax.ppermute(jnp.where(even, to_lo, to_hi), axis, outer)
    return jnp.where(even, second, first), jnp.where(even, first, second)


def local(state, source_in, counts, diffusivity, log_rate, activation, heat_release):
    nx = lax.axis_size("gx")
    ny = lax.axis_size("gy")
    rows, cx, cy, cz = state.shape
    cell_counts = jnp.broadcast_to(counts[:, :, None], (cx, cy, cz))

    to_xm = jnp.concatenate([state[:, :2], source_in[:, :1]], 1)
    to_xp = jnp.concatenate([state[:, cx - 2:], source_in[:, cx - 1:]], 1)
    from_xm, from_xp = exchange(to_xm, to_xp, "gx", nx)

    early = chemistry(state, cell_counts, log_rate, activation, heat_release)

    def zeros(a, b):
        return jnp.zeros((rows, a, b, cz), jnp.float32)

    wide = jnp.concatenate([from_xm[:, :2], state, from_xp[:, :2]], 1)
    wide_src = jnp.concatenate([from_xm[:, 2:], source_in, from_xp[:, 2:]], 1)
    to_ym = jnp.concatenate([wide[:, 1:-1, :2], wide_src[:, :, :1]], 2)
    to_yp = jnp.concatenate([wide[:, 1:-1, cy - 2:], wide_src[:, :, cy - 1:]], 2)
    from_ym, from_yp = exchange(to_ym, to_yp, "gy", ny)
    ext = jnp.concatenate(
        [
            jnp.concatenate([zeros(1, 2), wide[:, :1], zeros(1, 2)], 2),
            jnp.concatenate([from_ym[:, :, :2], wide[:, 1:-1], from_yp[:, :, :2]], 2),
            jnp.concatenate([zeros(1, 2), wide[:, -1:], zeros(1, 2)], 2),
        ],
        1,
    )
    src = jnp.concatenate([from_ym[:, :, 2:], wide_src, from_yp[:, :, 2:]], 2)
    next_state, late_source = finish(
        ext, src, early, cell_counts, diffusivity, log_rate, activation, heat_release
    )
    return (next_state, late_source)


def solution(mesh):
    in_specs = (
        P(None, "gx", "gy", None),
        P(None, "gx", "gy", None),
        P("gx", "gy"),
        P(),
        P(),
        P(),
        P(),
    )
    out_specs = (P(None, "gx", "gy", None), P(None, "gx", "gy", None))
    return jax.shard_map(local, mesh=mesh, in_specs=in_specs, out_specs=out_specs, check_vma=False)
```

```python
import jax
import jax.numpy as jnp
import numpy as np
from jax import lax
from jax.experimental import pallas as pl
from jax.experimental.pallas import tpu as pltpu
from jax.sharding import PartitionSpec as P

time_step = 0.15
reaction_table = (
    (3, 1, (4, 5)),
    (4, 0, (3, 5)),
    (5, 0, (3, 2)),
    (5, 5, (4, 2)),
    (3, 3, (0,)),
    (3, 5, (2,)),
    (4, 4, (1,)),
    (3, 4, (5,)),
    (3, 1, (6,)),
    (6, 3, (0, 1)),
    (6, 3, (5, 5)),
    (6, 4, (1, 5)),
    (6, 5, (2, 1)),
    (6, 6, (7, 1)),
    (7, 9, (5, 5)),
    (7, 3, (2, 5)),
    (7, 3, (6, 0)),
    (7, 4, (5, 6)),
    (7, 5, (6, 2)),
    (0, 9, (3, 3)),
    (2, 9, (3, 5)),
)
SPECIES = 9
CMAX = 8


def stoichiometry():
    change = np.zeros((SPECIES, len(reaction_table)), np.int64)
    for reaction, entry in enumerate(reaction_table):
        change[entry[0], reaction] -= 1
        if entry[1] < SPECIES:
            change[entry[1], reaction] -= 1
        for product in entry[2]:
            change[product, reaction] += 1
    return change


def react(start, cnt, rate_ref, act_ref, heat_ref):
    change = stoichiometry()
    reactions = len(reaction_table)
    temper = start[SPECIES]
    coeffs = [jnp.exp(rate_ref[r] - act_ref[r] / temper) for r in range(reactions)]
    heat = [heat_ref[r] for r in range(reactions)]
    stride = time_step / cnt.astype(jnp.float32)
    cur = list(start)
    for turn in range(CMAX):
        active = turn < cnt
        rates = []
        for r, entry in enumerate(reaction_table):
            term = coeffs[r] * cur[entry[0]]
            if entry[1] < SPECIES:
                term = term * cur[entry[1]]
            rates.append(term)
        new = []
        for s in range(SPECIES):
            total = None
            for r in range(reactions):
                c = int(change[s, r])
                if c == 0:
                    continue
                piece = rates[r] if abs(c) == 1 else rates[r] * float(abs(c))
                if total is None:
                    total = piece if c > 0 else -piece
                elif c > 0:
                    total = total + piece
                else:
                    total = total - piece
            if total is None:
                new.append(cur[s])
            else:
                new.append(jnp.where(active, cur[s] + stride * total, cur[s]))
        heat_total = heat[0] * rates[0]
        for r in range(1, reactions):
            heat_total = heat_total + heat[r] * rates[r]
        new.append(jnp.where(active, cur[SPECIES] + stride * heat_total, cur[SPECIES]))
        cur = new
    return [(cur[s] - start[s]) / time_step for s in range(len(start))]


def chem_kernel(rate_ref, act_ref, heat_ref, u_ref, cnt_ref, o_ref):
    rows = u_ref.shape[0]

    def per_x(x, carry):
        start = [u_ref[s, x] for s in range(rows)]
        out = react(start, cnt_ref[x], rate_ref, act_ref, heat_ref)
        for s in range(rows):
            o_ref[s, x] = out[s]
        return carry

    lax.fori_loop(0, u_ref.shape[1], per_x, 0)


def finish_kernel(
    diff_ref, rate_ref, act_ref, heat_ref, ext_ref, src_ref, early_ref, cnt_ref,
    next_ref, late_ref, first_ref,
):
    rows, cx, cy, _ = early_ref.shape
    lanes = ext_ref.shape[3]

    def laplace(centre, xm, xp, ym, yp):
        beside = xm + xp
        beside = beside + ym + yp
        beside = beside + pltpu.roll(centre, 1, 1) + pltpu.roll(centre, lanes - 1, 1)
        return beside - 6.0 * centre

    def first_row(i, carry, windows=(0, 2)):
        e = i + 1
        for r in range(rows):
            for lo in windows:
                centre = ext_ref[r, e, pl.ds(lo + 1, cy)]
                lap = laplace(
                    centre,
                    ext_ref[r, e - 1, pl.ds(lo + 1, cy)],
                    ext_ref[r, e + 1, pl.ds(lo + 1, cy)],
                    ext_ref[r, e, pl.ds(lo, cy)],
                    ext_ref[r, e, pl.ds(lo + 2, cy)],
                )
                first_ref[r, i, pl.ds(lo, cy)] = centre + time_step * (
                    diff_ref[r] * lap + src_ref[r, i, pl.ds(lo, cy)]
                )
        return carry

    first_row(0, 0, (1,))
    first_row(cx + 1, 0, (1,))
    lax.fori_loop(1, cx + 1, first_row, 0)

    def box_row(x, carry):
        start = []
        for r in range(rows):
            centre = first_ref[r, x + 1, pl.ds(1, cy)]
            lap = laplace(
                centre,
                first_ref[r, x, pl.ds(1, cy)],
                first_ref[r, x + 2, pl.ds(1, cy)],
                first_ref[r, x + 1, pl.ds(0, cy)],
                first_ref[r, x + 1, pl.ds(2, cy)],
            )
            state = ext_ref[r, x + 2, pl.ds(2, cy)]
            next_ref[r, x] = 0.5 * state + 0.5 * (
                centre + time_step * (diff_ref[r] * lap + early_ref[r, x])
            )
            start.append(centre)
        out = react(start, cnt_ref[x], rate_ref, act_ref, heat_ref)
        for r in range(rows):
            late_ref[r, x] = out[r]
        return carry

    lax.fori_loop(0, cx, box_row, 0)


def finish(ext, src, early, cell_counts, diffusivity, log_rate, activation, heat_release):
    rows, cx, cy, cz = early.shape
    smem = pl.BlockSpec(memory_space=pltpu.SMEM)
    vmem = pl.BlockSpec(memory_space=pltpu.VMEM)
    box = jax.ShapeDtypeStruct(early.shape, jnp.float32)
    return pl.pallas_call(
        finish_kernel,
        out_shape=(box, box),
        in_specs=[smem, smem, smem, smem, vmem, vmem, vmem, vmem],
        out_specs=(vmem, vmem),
        scratch_shapes=[pltpu.VMEM((rows, cx + 2, 2 * cy, cz), jnp.float32)],
    )(diffusivity, log_rate, activation, heat_release, ext, src, early, cell_counts)


def chemistry(fields, cell_counts, log_rate, activation, heat_release):
    smem = pl.BlockSpec(memory_space=pltpu.SMEM)
    vmem = pl.BlockSpec(memory_space=pltpu.VMEM)
    return pl.pallas_call(
        chem_kernel,
        out_shape=jax.ShapeDtypeStruct(fields.shape, jnp.float32),
        in_specs=[smem, smem, smem, vmem, vmem],
        out_specs=vmem,
    )(log_rate, activation, heat_release, fields, cell_counts)


def shift_pairs(size, step):
    return [(i, (i + step) % size) for i in range(size)]


def exchange(to_lo, to_hi, axis, size):
    if size % 2:
        from_lo = lax.ppermute(to_hi, axis, shift_pairs(size, 1))
        from_hi = lax.ppermute(to_lo, axis, shift_pairs(size, -1))
        return from_lo, from_hi
    even = lax.axis_index(axis) % 2 == 0
    inner = [(i, i + 1 if i % 2 == 0 else i - 1) for i in range(size)]
    outer = [(i, (i - 1) % size if i % 2 == 0 else (i + 1) % size) for i in range(size)]
    first = lax.ppermute(jnp.where(even, to_hi, to_lo), axis, inner)
    second = lax.ppermute(jnp.where(even, to_lo, to_hi), axis, outer)
    return jnp.where(even, second, first), jnp.where(even, first, second)


def local(state, source_in, counts, diffusivity, log_rate, activation, heat_release):
    nx = lax.axis_size("gx")
    ny = lax.axis_size("gy")
    rows, cx, cy, cz = state.shape
    cell_counts = jnp.broadcast_to(counts[:, :, None], (cx, cy, cz))

    to_xm = jnp.concatenate([state[:, :2], source_in[:, :1]], 1)
    to_xp = jnp.concatenate([state[:, cx - 2:], source_in[:, cx - 1:]], 1)
    from_xm, from_xp = exchange(to_xm, to_xp, "gx", nx)

    early = chemistry(state, cell_counts, log_rate, activation, heat_release)

    def zeros(a, b):
        return jnp.zeros((rows, a, b, cz), jnp.float32)

    wide = jnp.concatenate([from_xm[:, :2], state, from_xp[:, :2]], 1)
    wide_src = jnp.concatenate([from_xm[:, 2:], source_in, from_xp[:, 2:]], 1)
    to_ym = jnp.concatenate([wide[:, 1:-1, :2], wide_src[:, :, :1]], 2)
    to_yp = jnp.concatenate([wide[:, 1:-1, cy - 2:], wide_src[:, :, cy - 1:]], 2)
    from_ym, from_yp = exchange(to_ym, to_yp, "gy", ny)
    ext = jnp.concatenate(
        [
            jnp.concatenate([zeros(1, 2), wide[:, :1], zeros(1, 2)], 2),
            jnp.concatenate([from_ym[:, :, :2], wide[:, 1:-1], from_yp[:, :, :2]], 2),
            jnp.concatenate([zeros(1, 2), wide[:, -1:], zeros(1, 2)], 2),
        ],
        1,
    )
    src = jnp.concatenate([from_ym[:, :, 2:], wide_src, from_yp[:, :, 2:]], 2)
    next_state, late_source = finish(
        ext, src, early, cell_counts, diffusivity, log_rate, activation, heat_release
    )
    return (next_state, late_source)


def solution(mesh):
    in_specs = (
        P(None, "gx", "gy", None),
        P(None, "gx", "gy", None),
        P("gx", "gy"),
        P(),
        P(),
        P(),
        P(),
    )
    out_specs = (P(None, "gx", "gy", None), P(None, "gx", "gy", None))
    return jax.shard_map(local, mesh=mesh, in_specs=in_specs, out_specs=out_specs, check_vma=False)
```

```python
import jax
import jax.numpy as jnp
import numpy as np
from jax import lax
from jax.experimental import pallas as pl
from jax.experimental.pallas import tpu as pltpu
from jax.sharding import PartitionSpec as P

time_step = 0.15
reaction_table = (
    (3, 1, (4, 5)),
    (4, 0, (3, 5)),
    (5, 0, (3, 2)),
    (5, 5, (4, 2)),
    (3, 3, (0,)),
    (3, 5, (2,)),
    (4, 4, (1,)),
    (3, 4, (5,)),
    (3, 1, (6,)),
    (6, 3, (0, 1)),
    (6, 3, (5, 5)),
    (6, 4, (1, 5)),
    (6, 5, (2, 1)),
    (6, 6, (7, 1)),
    (7, 9, (5, 5)),
    (7, 3, (2, 5)),
    (7, 3, (6, 0)),
    (7, 4, (5, 6)),
    (7, 5, (6, 2)),
    (0, 9, (3, 3)),
    (2, 9, (3, 5)),
)
SPECIES = 9
CMAX = 8


def stoichiometry():
    change = np.zeros((SPECIES, len(reaction_table)), np.int64)
    for reaction, entry in enumerate(reaction_table):
        change[entry[0], reaction] -= 1
        if entry[1] < SPECIES:
            change[entry[1], reaction] -= 1
        for product in entry[2]:
            change[product, reaction] += 1
    return change


def react(start, cnt, rate_ref, act_ref, heat_ref):
    change = stoichiometry()
    reactions = len(reaction_table)
    temper = start[SPECIES]
    coeffs = [jnp.exp(rate_ref[r] - act_ref[r] / temper) for r in range(reactions)]
    heat = [heat_ref[r] for r in range(reactions)]
    stride = time_step / cnt.astype(jnp.float32)
    cur = list(start)
    for turn in range(CMAX):
        step = jnp.where(turn < cnt, stride, 0.0)
        rates = []
        for r, entry in enumerate(reaction_table):
            term = coeffs[r] * cur[entry[0]]
            if entry[1] < SPECIES:
                term = term * cur[entry[1]]
            rates.append(term)
        new = []
        for s in range(SPECIES):
            total = None
            for r in range(reactions):
                c = int(change[s, r])
                if c == 0:
                    continue
                piece = rates[r] if abs(c) == 1 else rates[r] * float(abs(c))
                if total is None:
                    total = piece if c > 0 else -piece
                elif c > 0:
                    total = total + piece
                else:
                    total = total - piece
            if total is None:
                new.append(cur[s])
            else:
                new.append(cur[s] + step * total)
        heat_total = heat[0] * rates[0]
        for r in range(1, reactions):
            heat_total = heat_total + heat[r] * rates[r]
        new.append(cur[SPECIES] + step * heat_total)
        cur = new
    return [(cur[s] - start[s]) / time_step for s in range(len(start))]


def chem_kernel(rate_ref, act_ref, heat_ref, u_ref, cnt_ref, o_ref):
    rows = u_ref.shape[0]

    def per_x(x, carry):
        start = [u_ref[s, x] for s in range(rows)]
        out = react(start, cnt_ref[x], rate_ref, act_ref, heat_ref)
        for s in range(rows):
            o_ref[s, x] = out[s]
        return carry

    lax.fori_loop(0, u_ref.shape[1], per_x, 0)


def finish_kernel(
    diff_ref, rate_ref, act_ref, heat_ref, ext_ref, src_ref, early_ref, cnt_ref,
    next_ref, late_ref, first_ref,
):
    rows, cx, cy, _ = early_ref.shape
    lanes = ext_ref.shape[3]

    def laplace(centre, xm, xp, ym, yp):
        beside = xm + xp
        beside = beside + ym + yp
        beside = beside + pltpu.roll(centre, 1, 1) + pltpu.roll(centre, lanes - 1, 1)
        return beside - 6.0 * centre

    def first_row(i, carry, windows=(0, 2)):
        e = i + 1
        for r in range(rows):
            for lo in windows:
                centre = ext_ref[r, e, pl.ds(lo + 1, cy)]
                lap = laplace(
                    centre,
                    ext_ref[r, e - 1, pl.ds(lo + 1, cy)],
                    ext_ref[r, e + 1, pl.ds(lo + 1, cy)],
                    ext_ref[r, e, pl.ds(lo, cy)],
                    ext_ref[r, e, pl.ds(lo + 2, cy)],
                )
                first_ref[r, i, pl.ds(lo, cy)] = centre + time_step * (
                    diff_ref[r] * lap + src_ref[r, i, pl.ds(lo, cy)]
                )
        return carry

    first_row(0, 0, (1,))
    first_row(cx + 1, 0, (1,))
    lax.fori_loop(1, cx + 1, first_row, 0)

    def box_row(x, carry):
        start = []
        for r in range(rows):
            centre = first_ref[r, x + 1, pl.ds(1, cy)]
            lap = laplace(
                centre,
                first_ref[r, x, pl.ds(1, cy)],
                first_ref[r, x + 2, pl.ds(1, cy)],
                first_ref[r, x + 1, pl.ds(0, cy)],
                first_ref[r, x + 1, pl.ds(2, cy)],
            )
            state = ext_ref[r, x + 2, pl.ds(2, cy)]
            next_ref[r, x] = 0.5 * state + 0.5 * (
                centre + time_step * (diff_ref[r] * lap + early_ref[r, x])
            )
            start.append(centre)
        out = react(start, cnt_ref[x], rate_ref, act_ref, heat_ref)
        for r in range(rows):
            late_ref[r, x] = out[r]
        return carry

    lax.fori_loop(0, cx, box_row, 0)


def finish(ext, src, early, cell_counts, diffusivity, log_rate, activation, heat_release):
    rows, cx, cy, cz = early.shape
    smem = pl.BlockSpec(memory_space=pltpu.SMEM)
    vmem = pl.BlockSpec(memory_space=pltpu.VMEM)
    box = jax.ShapeDtypeStruct(early.shape, jnp.float32)
    return pl.pallas_call(
        finish_kernel,
        out_shape=(box, box),
        in_specs=[smem, smem, smem, smem, vmem, vmem, vmem, vmem],
        out_specs=(vmem, vmem),
        scratch_shapes=[pltpu.VMEM((rows, cx + 2, 2 * cy, cz), jnp.float32)],
    )(diffusivity, log_rate, activation, heat_release, ext, src, early, cell_counts)


def chemistry(fields, cell_counts, log_rate, activation, heat_release):
    smem = pl.BlockSpec(memory_space=pltpu.SMEM)
    vmem = pl.BlockSpec(memory_space=pltpu.VMEM)
    return pl.pallas_call(
        chem_kernel,
        out_shape=jax.ShapeDtypeStruct(fields.shape, jnp.float32),
        in_specs=[smem, smem, smem, vmem, vmem],
        out_specs=vmem,
    )(log_rate, activation, heat_release, fields, cell_counts)


def shift_pairs(size, step):
    return [(i, (i + step) % size) for i in range(size)]


def exchange(to_lo, to_hi, axis, size):
    if size % 2:
        from_lo = lax.ppermute(to_hi, axis, shift_pairs(size, 1))
        from_hi = lax.ppermute(to_lo, axis, shift_pairs(size, -1))
        return from_lo, from_hi
    even = lax.axis_index(axis) % 2 == 0
    inner = [(i, i + 1 if i % 2 == 0 else i - 1) for i in range(size)]
    outer = [(i, (i - 1) % size if i % 2 == 0 else (i + 1) % size) for i in range(size)]
    first = lax.ppermute(jnp.where(even, to_hi, to_lo), axis, inner)
    second = lax.ppermute(jnp.where(even, to_lo, to_hi), axis, outer)
    return jnp.where(even, second, first), jnp.where(even, first, second)


def local(state, source_in, counts, diffusivity, log_rate, activation, heat_release):
    nx = lax.axis_size("gx")
    ny = lax.axis_size("gy")
    rows, cx, cy, cz = state.shape
    cell_counts = jnp.broadcast_to(counts[:, :, None], (cx, cy, cz))

    to_xm = jnp.concatenate([state[:, :2], source_in[:, :1]], 1)
    to_xp = jnp.concatenate([state[:, cx - 2:], source_in[:, cx - 1:]], 1)
    from_xm, from_xp = exchange(to_xm, to_xp, "gx", nx)

    early = chemistry(state, cell_counts, log_rate, activation, heat_release)

    def zeros(a, b):
        return jnp.zeros((rows, a, b, cz), jnp.float32)

    wide = jnp.concatenate([from_xm[:, :2], state, from_xp[:, :2]], 1)
    wide_src = jnp.concatenate([from_xm[:, 2:], source_in, from_xp[:, 2:]], 1)
    to_ym = jnp.concatenate([wide[:, 1:-1, :2], wide_src[:, :, :1]], 2)
    to_yp = jnp.concatenate([wide[:, 1:-1, cy - 2:], wide_src[:, :, cy - 1:]], 2)
    from_ym, from_yp = exchange(to_ym, to_yp, "gy", ny)
    ext = jnp.concatenate(
        [
            jnp.concatenate([zeros(1, 2), wide[:, :1], zeros(1, 2)], 2),
            jnp.concatenate([from_ym[:, :, :2], wide[:, 1:-1], from_yp[:, :, :2]], 2),
            jnp.concatenate([zeros(1, 2), wide[:, -1:], zeros(1, 2)], 2),
        ],
        1,
    )
    src = jnp.concatenate([from_ym[:, :, 2:], wide_src, from_yp[:, :, 2:]], 2)
    next_state, late_source = finish(
        ext, src, early, cell_counts, diffusivity, log_rate, activation, heat_release
    )
    return (next_state, late_source)


def solution(mesh):
    in_specs = (
        P(None, "gx", "gy", None),
        P(None, "gx", "gy", None),
        P("gx", "gy"),
        P(),
        P(),
        P(),
        P(),
    )
    out_specs = (P(None, "gx", "gy", None), P(None, "gx", "gy", None))
    return jax.shard_map(local, mesh=mesh, in_specs=in_specs, out_specs=out_specs, check_vma=False)
```
